512 devices in a mesh: seq: 64 (over y, z_lo, x), ch: 8 (over z_hi, core).
Axes of the slice: x: 4, y: 8, z: 8 (z_hi: 4, z_lo: 2; z = z_hi * 2 + z_lo), core: 2. Of those that a mesh axis runs over, the one named last changes fastest.
Arguments:
- inputs: bfloat16 [16384, 1024], P('seq', 'ch'), may hold values from -6 to 6
- gate_values: bfloat16 [16384, 1024], P('seq', 'ch'), may hold values from -600 to 1100
- causal_filter: bfloat16 [16384, 1024], P('seq', 'ch'), may hold values from -0.046875 to 0.046875
- anti_filter: bfloat16 [16384, 1024], P('seq', 'ch'), may hold values from -0.046875 to 0.046875
- skip_gain: float32 [1024], P('ch'), may hold values from 0.25 to 1.75
- norm_gain: float32 [1024], P('ch'), may hold values from 0.25 to 1.75
Outputs:
- mixer_out: bfloat16 [16384, 1024], P('seq', 'ch')
The draws below stay inside these ranges and needn't reach their ends.
All inputs are finite; a program needn't handle non-finite values.
Results may differ from the reference program's by a relative error of at most 0.007.
Values may be sent and summed in bfloat16 or wider, within the bound.
No kernel may reach another device: no remote copies, remote signals or barrier semaphores. Data moves between devices by JAX's collectives and lax.ppermute only.
A program may use at most 128 MiB of HBM per device.

```python
import math
import jax
import jax.numpy as jnp
from jax import lax

D = 1024
TOK_DEV = 256
LEN = 16384
N_SEQ = 64


def draw_gate_values(key, part):
    noise_key = jax.random.fold_in(key, 11)
    row_key = jax.random.fold_in(key, 12)
    column_ids = jnp.arange(D, dtype=jnp.float32) / jnp.float32(D - 1)
    noise_vals = jnp.clip(jax.random.normal(noise_key, (LEN, D), jnp.float32), -4.0, 4.0)
    row_scale = jnp.exp(jax.random.uniform(row_key, (LEN, 1), jnp.float32, 0.0, math.log(10.0)))
    col_scale = jnp.exp(column_ids * math.log(10.0))
    return (noise_vals * row_scale * col_scale[None, :]).astype(jnp.bfloat16)


def block_scale(key, dims, cuts, least, top_value):
    def one(axis_at, blocks):
        draws = jax.random.uniform(jax.random.fold_in(jax.random.fold_in(key, 6), axis_at), (blocks,), jnp.float32, least / len(cuts), top_value / len(cuts))
        return jnp.repeat(jnp.exp(draws), dims[axis_at] // blocks).reshape((-1,) + (1,) * (len(dims) - axis_at - 1))

    level = one(*cuts[0])
    for cut in cuts[1:]:
        level = level * one(*cut)
    return level


def noise(own_key, dims, width, most, cuts=(), kind=jnp.bfloat16):
    drawn = width * jax.random.normal(own_key, dims, jnp.float32)
    if cuts:
        drawn = drawn * block_scale(own_key, dims, cuts, -0.22, 0.18)
    return jnp.clip(drawn, -most, most).astype(kind)


def setup_inputs(seed: int = 0) -> dict:
    seeds = jax.random.split(jax.random.key(seed), 7)
    inputs = noise(seeds[0], (LEN, D), 1.0, 6.0, ((0, 64), (1, 8)))
    gate_values = draw_gate_values(jax.random.fold_in(seeds[6], 71), 0)
    causal_filter = noise(seeds[2], (LEN, D), LEN ** -0.5, 0.046875, ((0, 64), (1, 8)))
    anti_filter = noise(seeds[3], (LEN, D), LEN ** -0.5, 0.046875, ((0, 64), (1, 8)))
    skip_gain = jnp.clip(1.0 + 0.15 * jax.random.normal(seeds[4], (D,), jnp.float32), 0.25, 1.75)
    norm_gain = jnp.clip(1.0 + 0.15 * jax.random.normal(seeds[5], (D,), jnp.float32), 0.25, 1.75)
    return dict(inputs=inputs, gate_values=gate_values, causal_filter=causal_filter, anti_filter=anti_filter, skip_gain=skip_gain, norm_gain=norm_gain)


def forward_table(rows_dev):
    freq_ids = jnp.arange(rows_dev + 1, dtype=jnp.int32)[:, None]
    place_ids = jnp.arange(rows_dev, dtype=jnp.int32)[None, :]
    phases = (freq_ids * place_ids % (2 * rows_dev)).astype(jnp.float32) * jnp.float32(math.pi / rows_dev)
    return jnp.concatenate([jnp.cos(phases), -jnp.sin(phases)], axis=0).astype(jnp.bfloat16)

def inverse_table(rows_dev):
    place_ids = jnp.arange(rows_dev, dtype=jnp.int32)[:, None] + rows_dev
    freq_ids = jnp.arange(rows_dev + 1, dtype=jnp.int32)[None, :]
    phases = (freq_ids * place_ids % (2 * rows_dev)).astype(jnp.float32) * jnp.float32(math.pi / rows_dev)
    edges = jnp.logical_or(freq_ids == 0, freq_ids == rows_dev)
    weights = jnp.where(edges, jnp.float32(1.0), jnp.float32(2.0)) / jnp.float32(2 * rows_dev)
    return jnp.concatenate([weights * jnp.cos(phases), -weights * jnp.sin(phases)], axis=1)

def alternating(rows_dev):
    parity = (jnp.arange(rows_dev + 1, dtype=jnp.int32) % 2).astype(jnp.float32)
    signs_half = jnp.float32(1.0) - jnp.float32(2.0) * parity
    return jnp.concatenate([signs_half, signs_half])[:, None]

def complex_product(segment, block_spec, conj_sign):
    freq_rows = segment.shape[-2] // 2
    seg_re = segment[..., :freq_rows, :]
    seg_im = segment[..., freq_rows:, :] * conj_sign
    blk_re = block_spec[..., :freq_rows, :]
    blk_im = block_spec[..., freq_rows:, :]
    return jnp.concatenate([seg_re * blk_re - seg_im * blk_im, seg_re * blk_im + seg_im * blk_re], axis=-2)

def spectra_of(forward_lookup, series):
    block_pieces = series.astype(jnp.float32).reshape(N_SEQ, TOK_DEV, D)
    filter_spectra = jnp.einsum('bk,gkt->gbt', forward_lookup.astype(jnp.float32), block_pieces, precision=lax.Precision.HIGHEST)
    return lax.optimization_barrier(filter_spectra.astype(jnp.bfloat16)).astype(jnp.float32)

def segments_for(filter_spectra, alternate):
    lower_spec = jnp.concatenate([jnp.zeros_like(filter_spectra[:1]), filter_spectra[:-1]], axis=0)
    return lower_spec + alternate[None] * filter_spectra

def reference(inputs, gate_values, causal_filter, anti_filter, skip_gain, norm_gain):
    forward_lookup = forward_table(TOK_DEV)
    inv_table = inverse_table(TOK_DEV)
    alternate = alternating(TOK_DEV)
    row_ids = jnp.arange(LEN, dtype=jnp.int32)[:, None]
    anti_masked = jnp.where(row_ids > 0, anti_filter, jnp.zeros_like(anti_filter))
    input_spec = spectra_of(forward_lookup, inputs)
    causal_seg = segments_for(spectra_of(forward_lookup, causal_filter), alternate)
    anti_seg = segments_for(spectra_of(forward_lookup, anti_masked), alternate)
    margin = jnp.zeros_like(input_spec)
    padded = jnp.concatenate([margin, input_spec, margin], axis=0)

    def lag_term(lag_idx, spectrum_sum):
        lag_now = jnp.asarray(lag_idx).astype(jnp.int32)
        earlier = lax.dynamic_slice_in_dim(padded, jnp.int32(N_SEQ) - lag_now, N_SEQ, 0)
        later_spec = lax.dynamic_slice_in_dim(padded, jnp.int32(N_SEQ) + lag_now, N_SEQ, 0)
        causal_now = lax.dynamic_slice_in_dim(causal_seg, lag_now, 1, 0)
        anti_now = lax.dynamic_slice_in_dim(anti_seg, lag_now, 1, 0)
        spectrum_sum = spectrum_sum + complex_product(causal_now, earlier, jnp.float32(1.0))
        return spectrum_sum + complex_product(anti_now, later_spec, jnp.float32(-1.0))
    spectrum_sum = lax.fori_loop(0, N_SEQ, lag_term, jnp.zeros_like(input_spec))
    convolved = jnp.einsum('tf,pfd->ptd', inv_table, spectrum_sum, precision=lax.Precision.HIGHEST).reshape(LEN, D)
    mixed = gate_values.astype(jnp.float32) * (convolved + skip_gain[None, :] * inputs.astype(jnp.float32))
    mean_square = lax.optimization_barrier(jnp.mean(mixed * mixed, axis=1, keepdims=True))
    return (norm_gain[None, :] * mixed * lax.rsqrt(mean_square + 1e-06)).astype(jnp.bfloat16)
```

```python
import numpy as np

import jax
import jax.numpy as jnp
from jax import lax
from jax.sharding import PartitionSpec as P

D = 1024
HIGHEST = lax.Precision.HIGHEST


def padded(count, unit=8):
    return -(-count // unit) * unit


def inner_tables(rows_dev):
    freqs = rows_dev + 1
    fp = padded(freqs)
    f = np.arange(freqs)[:, None]
    n = np.arange(rows_dev)[None, :]
    phase = ((f * n) % (2 * rows_dev)) * (np.pi / rows_dev)
    fwd = np.zeros((2 * fp, rows_dev))
    fwd[:freqs] = np.cos(phase)
    fwd[fp : fp + freqs] = -np.sin(phase)
    t = np.arange(rows_dev)[:, None] + rows_dev
    f2 = np.arange(freqs)[None, :]
    phase2 = ((f2 * t) % (2 * rows_dev)) * (np.pi / rows_dev)
    weight = np.where((f2 == 0) | (f2 == rows_dev), 1.0, 2.0) / (2 * rows_dev)
    inv = np.zeros((rows_dev, 2 * fp))
    inv[:, :freqs] = weight * np.cos(phase2)
    inv[:, fp : fp + freqs] = -weight * np.sin(phase2)
    return fp, fwd, inv


def outer_tables(blocks, fp):
    size = 2 * blocks
    j = np.arange(blocks)[:, None]
    m = np.arange(size)[None, :]
    phase = 2 * np.pi * ((j * m) % size) / size
    fwd = np.concatenate([np.cos(phase), np.sin(phase)], axis=1)
    mi = np.arange(size)[:, None]
    i = np.arange(blocks)[None, :]
    phase_i = 2 * np.pi * ((mi * i) % size) / size
    cos_i = np.cos(phase_i) / size
    sin_i = np.sin(phase_i) / size
    inv_re = np.concatenate([cos_i, -sin_i], axis=0)
    inv_im = np.concatenate([sin_i, cos_i], axis=0)
    sign = np.where(np.arange(fp) % 2 == 0, 1.0, -1.0)[:, None]
    step = 2 * np.pi * np.arange(size)[None, :] / size
    shift_re = np.cos(step) + sign
    shift_im = -np.sin(step) + 0.0 * sign
    return fwd, inv_re, inv_im, shift_re, shift_im


def on_device(inputs, gate_values, causal_filter, anti_filter, skip_gain, norm_gain):
    rows_dev, chan_dev = inputs.shape
    blocks = lax.axis_size("seq")
    per = chan_dev // blocks
    size = 2 * blocks
    f32 = jnp.float32
    own_index = lax.axis_index("seq")
    row_ids = lax.broadcasted_iota(jnp.int32, (rows_dev, 1), 0) + own_index * rows_dev
    anti_masked = jnp.where(row_ids > 0, anti_filter, jnp.zeros_like(anti_filter))

    fp, fwd_np, inv_np = inner_tables(rows_dev)
    ofwd_np, oinv_re_np, oinv_im_np, sh_re_np, sh_im_np = outer_tables(blocks, fp)
    fwd = jnp.asarray(fwd_np, jnp.bfloat16)
    inv = jnp.asarray(inv_np, f32)
    ofwd = jnp.asarray(ofwd_np, f32)
    oinv_re = jnp.asarray(oinv_re_np, f32)
    oinv_im = jnp.asarray(oinv_im_np, f32)
    sh_re = jnp.asarray(sh_re_np, f32)
    sh_im = jnp.asarray(sh_im_np, f32)

    stacked = jnp.stack([inputs, causal_filter, anti_masked])
    send = (
        stacked.reshape(3, rows_dev, blocks, per)
        .transpose(2, 0, 3, 1)
        .reshape(blocks, 3 * per * rows_dev)
    )
    recv = lax.all_to_all(send, "seq", 0, 0, tiled=True)
    series = recv.reshape(blocks, 3 * per, rows_dev).transpose(1, 0, 2)

    spec = jnp.einsum("fn,qbn->qfb", fwd, series, preferred_element_type=f32)
    spec = spec.astype(jnp.bfloat16).astype(f32)
    z = jnp.einsum("qfb,bk->qfk", spec, ofwd, precision=HIGHEST, preferred_element_type=f32)
    z_re, z_im = z[:, :fp], z[:, fp:]
    x_re = (z_re[..., :size] + z_im[..., size:]).reshape(3, per, fp, size)
    x_im = (z_im[..., :size] - z_re[..., size:]).reshape(3, per, fp, size)

    c_re = sh_re * x_re[1] - sh_im * x_im[1]
    c_im = sh_re * x_im[1] + sh_im * x_re[1]
    a_re = sh_re * x_re[2] - sh_im * x_im[2]
    a_im = sh_re * x_im[2] + sh_im * x_re[2]
    k_re = c_re + a_re
    k_im = c_im - a_im
    y_re = k_re * x_re[0] - k_im * x_im[0]
    y_im = k_re * x_im[0] + k_im * x_re[0]
    y_cat = jnp.concatenate([y_re, y_im], axis=-1)

    t_re = jnp.einsum("cfk,ki->cfi", y_cat, oinv_re, precision=HIGHEST, preferred_element_type=f32)
    t_im = jnp.einsum("cfk,ki->cfi", y_cat, oinv_im, precision=HIGHEST, preferred_element_type=f32)
    total = jnp.concatenate([t_re, t_im], axis=1)
    conv_t = jnp.einsum("cfi,tf->cit", total, inv, precision=HIGHEST, preferred_element_type=f32)

    back = conv_t.transpose(1, 0, 2).reshape(blocks, per * rows_dev)
    got = lax.all_to_all(back, "seq", 0, 0, tiled=True)
    convolved = got.reshape(blocks * per, rows_dev).T

    gated_mix = gate_values.astype(f32) * (convolved + skip_gain[None, :] * inputs.astype(f32))
    squares = lax.psum(jnp.sum(gated_mix * gated_mix, axis=1), "ch")
    inv_norm = lax.rsqrt(squares / D + 1e-06)
    return (norm_gain[None, :] * gated_mix * inv_norm[:, None]).astype(jnp.bfloat16)


def solution(mesh):
    placed = (P("seq", "ch"), P("seq", "ch"), P("seq", "ch"), P("seq", "ch"), P("ch"), P("ch"))
    return jax.shard_map(
        on_device, mesh=mesh, in_specs=placed, out_specs=P("seq", "ch"), check_vma=False
    )
```

```python
import numpy as np

import jax
import jax.numpy as jnp
from jax import lax
from jax.sharding import PartitionSpec as P

D = 1024
HIGHEST = lax.Precision.HIGHEST


def padded(count, unit=8):
    return -(-count // unit) * unit


def inner_tables(rows_dev):
    freqs = rows_dev + 1
    fp = padded(freqs)
    f = np.arange(freqs)[:, None]
    n = np.arange(rows_dev)[None, :]
    phase = ((f * n) % (2 * rows_dev)) * (np.pi / rows_dev)
    fwd = np.zeros((2 * fp, rows_dev))
    fwd[:freqs] = np.cos(phase)
    fwd[fp : fp + freqs] = -np.sin(phase)
    t = np.arange(rows_dev)[:, None] + rows_dev
    f2 = np.arange(freqs)[None, :]
    phase2 = ((f2 * t) % (2 * rows_dev)) * (np.pi / rows_dev)
    weight = np.where((f2 == 0) | (f2 == rows_dev), 1.0, 2.0) / (2 * rows_dev)
    inv = np.zeros((rows_dev, 2 * fp))
    inv[:, :freqs] = weight * np.cos(phase2)
    inv[:, fp : fp + freqs] = -weight * np.sin(phase2)
    return fp, fwd, inv


def outer_tables(blocks, fp):
    size = 2 * blocks
    j = np.arange(blocks)[:, None]
    m = np.arange(size)[None, :]
    phase = 2 * np.pi * ((j * m) % size) / size
    fwd = np.concatenate([np.cos(phase), np.sin(phase)], axis=1)
    mi = np.arange(size)[:, None]
    i = np.arange(blocks)[None, :]
    phase_i = 2 * np.pi * ((mi * i) % size) / size
    cos_i = np.cos(phase_i) / size
    sin_i = np.sin(phase_i) / size
    inv_re = np.concatenate([cos_i, -sin_i], axis=0)
    inv_im = np.concatenate([sin_i, cos_i], axis=0)
    sign = np.where(np.arange(fp) % 2 == 0, 1.0, -1.0)[:, None]
    step = 2 * np.pi * np.arange(size)[None, :] / size
    shift_re = np.cos(step) + sign
    shift_im = -np.sin(step) + 0.0 * sign
    return fwd, inv_re, inv_im, shift_re, shift_im


def on_device(inputs, gate_values, causal_filter, anti_filter, skip_gain, norm_gain):
    rows_dev, chan_dev = inputs.shape
    blocks = lax.axis_size("seq")
    per = chan_dev // blocks
    size = 2 * blocks
    f32 = jnp.float32
    own_index = lax.axis_index("seq")
    row_ids = lax.broadcasted_iota(jnp.int32, (rows_dev, 1), 0) + own_index * rows_dev
    anti_masked = jnp.where(row_ids > 0, anti_filter, jnp.zeros_like(anti_filter))

    fp, fwd_np, inv_np = inner_tables(rows_dev)
    ofwd_np, oinv_re_np, oinv_im_np, sh_re_np, sh_im_np = outer_tables(blocks, fp)
    fwd = jnp.asarray(fwd_np, jnp.bfloat16)
    inv = jnp.asarray(inv_np, f32)
    ofwd = jnp.asarray(ofwd_np, f32)
    oinv_re = jnp.asarray(oinv_re_np, f32)
    oinv_im = jnp.asarray(oinv_im_np, f32)
    sh_re = jnp.asarray(sh_re_np, f32)
    sh_im = jnp.asarray(sh_im_np, f32)

    stacked = jnp.stack([inputs, causal_filter, anti_masked])
    send = (
        stacked.reshape(3, rows_dev, blocks, per)
        .transpose(2, 0, 3, 1)
        .reshape(blocks, 3 * per * rows_dev)
    )
    recv = lax.all_to_all(send, "seq", 0, 0, tiled=True)
    series = recv.reshape(blocks, 3 * per, rows_dev).transpose(1, 0, 2)

    spec = jnp.einsum("fn,qbn->qfb", fwd, series, preferred_element_type=f32)
    spec = spec.astype(jnp.bfloat16).astype(f32)
    z = jnp.einsum("qfb,bk->qfk", spec, ofwd, precision=HIGHEST, preferred_element_type=f32)
    z_re, z_im = z[:, :fp], z[:, fp:]
    x_re = (z_re[..., :size] + z_im[..., size:]).reshape(3, per, fp, size)
    x_im = (z_im[..., :size] - z_re[..., size:]).reshape(3, per, fp, size)

    c_re = sh_re * x_re[1] - sh_im * x_im[1]
    c_im = sh_re * x_im[1] + sh_im * x_re[1]
    a_re = sh_re * x_re[2] - sh_im * x_im[2]
    a_im = sh_re * x_im[2] + sh_im * x_re[2]
    k_re = c_re + a_re
    k_im = c_im - a_im
    y_re = k_re * x_re[0] - k_im * x_im[0]
    y_im = k_re * x_im[0] + k_im * x_re[0]
    y_cat = jnp.concatenate([y_re, y_im], axis=-1)

    t_re = jnp.einsum("cfk,ki->cfi", y_cat, oinv_re, precision=HIGHEST, preferred_element_type=f32)
    t_im = jnp.einsum("cfk,ki->cfi", y_cat, oinv_im, precision=HIGHEST, preferred_element_type=f32)
    total = jnp.concatenate([t_re, t_im], axis=1)
    conv_t = jnp.einsum("cfi,tf->cit", total, inv, precision=HIGHEST, preferred_element_type=f32)

    back = conv_t.transpose(1, 0, 2).reshape(blocks, per * rows_dev)
    got = lax.all_to_all(back, "seq", 0, 0, tiled=True)
    convolved = got.reshape(blocks * per, rows_dev).T

    gated_mix = gate_values.astype(f32) * (convolved + skip_gain[None, :] * inputs.astype(f32))
    partial = jnp.sum(gated_mix * gated_mix, axis=1)
    squares = jnp.sum(lax.all_gather(partial, "ch", axis=0, tiled=False), axis=0)
    inv_norm = lax.rsqrt(squares / D + 1e-06)
    return (norm_gain[None, :] * gated_mix * inv_norm[:, None]).astype(jnp.bfloat16)


def solution(mesh):
    placed = (P("seq", "ch"), P("seq", "ch"), P("seq", "ch"), P("seq", "ch"), P("ch"), P("ch"))
    return jax.shard_map(
        on_device, mesh=mesh, in_specs=placed, out_specs=P("seq", "ch"), check_vma=False
    )
```

```python
import numpy as np

import jax
import jax.numpy as jnp
from jax import lax
from jax.sharding import PartitionSpec as P

D = 1024
HIGHEST = lax.Precision.HIGHEST


def padded(count, unit=8):
    return -(-count // unit) * unit


def inner_tables(rows_dev):
    freqs = rows_dev + 1
    fp = padded(freqs)
    f = np.arange(freqs)[:, None]
    n = np.arange(rows_dev)[None, :]
    phase = ((f * n) % (2 * rows_dev)) * (np.pi / rows_dev)
    fwd = np.zeros((2 * fp, rows_dev))
    fwd[:freqs] = np.cos(phase)
    fwd[fp : fp + freqs] = -np.sin(phase)
    t = np.arange(rows_dev)[:, None] + rows_dev
    f2 = np.arange(freqs)[None, :]
    phase2 = ((f2 * t) % (2 * rows_dev)) * (np.pi / rows_dev)
    weight = np.where((f2 == 0) | (f2 == rows_dev), 1.0, 2.0) / (2 * rows_dev)
    inv = np.zeros((rows_dev, 2 * fp))
    inv[:, :freqs] = weight * np.cos(phase2)
    inv[:, fp : fp + freqs] = -weight * np.sin(phase2)
    return fp, fwd, inv


def outer_tables(blocks, fp):
    size = 2 * blocks
    j = np.arange(blocks)[:, None]
    m = np.arange(size)[None, :]
    phase = 2 * np.pi * ((j * m) % size) / size
    fwd = np.concatenate([np.cos(phase), np.sin(phase)], axis=1)
    mi = np.arange(size)[:, None]
    i = np.arange(blocks)[None, :]
    phase_i = 2 * np.pi * ((mi * i) % size) / size
    cos_i = np.cos(phase_i) / size
    sin_i = np.sin(phase_i) / size
    inv_re = np.concatenate([cos_i, -sin_i], axis=0)
    inv_im = np.concatenate([sin_i, cos_i], axis=0)
    sign = np.where(np.arange(fp) % 2 == 0, 1.0, -1.0)[:, None]
    step = 2 * np.pi * np.arange(size)[None, :] / size
    shift_re = np.cos(step) + sign
    shift_im = -np.sin(step) + 0.0 * sign
    return fwd, inv_re, inv_im, shift_re, shift_im


def on_device(inputs, gate_values, causal_filter, anti_filter, skip_gain, norm_gain):
    rows_dev, chan_dev = inputs.shape
    blocks = lax.axis_size("seq")
    per = chan_dev // blocks
    size = 2 * blocks
    f32 = jnp.float32
    own_index = lax.axis_index("seq")

    fp, fwd_np, inv_np = inner_tables(rows_dev)
    ofwd_np, oinv_re_np, oinv_im_np, sh_re_np, sh_im_np = outer_tables(blocks, fp)
    fwd = jnp.asarray(fwd_np, jnp.bfloat16)
    inv = jnp.asarray(inv_np, f32)
    ofwd = jnp.asarray(ofwd_np, f32)
    oinv_re = jnp.asarray(oinv_re_np, f32)
    oinv_im = jnp.asarray(oinv_im_np, f32)
    sh_re = jnp.asarray(sh_re_np, f32)
    sh_im = jnp.asarray(sh_im_np, f32)

    stacked = jnp.stack([inputs, causal_filter, anti_filter, gate_values])
    lanes = 128
    send = (
        stacked.reshape(4, rows_dev, blocks, per)
        .transpose(2, 0, 3, 1)
        .reshape(blocks, 4 * per * rows_dev // lanes, lanes)
    )
    recv = lax.all_to_all(send, "seq", 0, 0, tiled=True)
    series = recv.reshape(blocks, 4, per, rows_dev)
    block_ids = lax.broadcasted_iota(jnp.int32, (blocks, 1, rows_dev), 0)
    tok_ids = lax.broadcasted_iota(jnp.int32, (blocks, 1, rows_dev), 2)
    first_row = jnp.logical_and(block_ids == 0, tok_ids == 0)
    anti_rows = jnp.where(first_row, jnp.zeros_like(series[:, 2]), series[:, 2])
    conv_in = jnp.stack([series[:, 0], series[:, 1], anti_rows], axis=1)
    conv_in = conv_in.reshape(blocks, 3 * per, rows_dev).transpose(1, 0, 2)

    spec = jnp.einsum("fn,qbn->qfb", fwd, conv_in, preferred_element_type=f32)
    spec = spec.astype(jnp.bfloat16).astype(f32)
    z = jnp.einsum("qfb,bk->qfk", spec, ofwd, precision=HIGHEST, preferred_element_type=f32)
    z_re, z_im = z[:, :fp], z[:, fp:]
    x_re = (z_re[..., :size] + z_im[..., size:]).reshape(3, per, fp, size)
    x_im = (z_im[..., :size] - z_re[..., size:]).reshape(3, per, fp, size)

    c_re = sh_re * x_re[1] - sh_im * x_im[1]
    c_im = sh_re * x_im[1] + sh_im * x_re[1]
    a_re = sh_re * x_re[2] - sh_im * x_im[2]
    a_im = sh_re * x_im[2] + sh_im * x_re[2]
    k_re = c_re + a_re
    k_im = c_im - a_im
    y_re = k_re * x_re[0] - k_im * x_im[0]
    y_im = k_re * x_im[0] + k_im * x_re[0]
    y_cat = jnp.concatenate([y_re, y_im], axis=-1)

    t_re = jnp.einsum("cfk,ki->cfi", y_cat, oinv_re, precision=HIGHEST, preferred_element_type=f32)
    t_im = jnp.einsum("cfk,ki->cfi", y_cat, oinv_im, precision=HIGHEST, preferred_element_type=f32)
    total = jnp.concatenate([t_re, t_im], axis=1)
    conv_t = jnp.einsum("cfi,tf->ict", total, inv, precision=HIGHEST, preferred_element_type=f32)

    skip_here = lax.dynamic_slice_in_dim(skip_gain, own_index * per, per)
    mixed_local = series[:, 3].astype(f32) * (
        conv_t + skip_here[None, :, None] * series[:, 0].astype(f32)
    )
    back = mixed_local.reshape(blocks, per * rows_dev // lanes, lanes)
    got = lax.all_to_all(back, "seq", 0, 0, tiled=True)
    gated_mix = got.reshape(blocks * per, rows_dev).T

    partial = jnp.sum(gated_mix * gated_mix, axis=1)
    squares = jnp.sum(lax.all_gather(partial, "ch", axis=0, tiled=False), axis=0)
    inv_norm = lax.rsqrt(squares / D + 1e-06)
    return (norm_gain[None, :] * gated_mix * inv_norm[:, None]).astype(jnp.bfloat16)


def solution(mesh):
    placed = (P("seq", "ch"), P("seq", "ch"), P("seq", "ch"), P("seq", "ch"), P("ch"), P("ch"))
    return jax.shard_map(
        on_device, mesh=mesh, in_specs=placed, out_specs=P("seq", "ch"), check_vma=False
    )
```

```python
import numpy as np

import jax
import jax.numpy as jnp
from jax import lax
from jax.sharding import PartitionSpec as P

D = 1024
HIGHEST = lax.Precision.HIGHEST


def padded(count, unit=8):
    return -(-count // unit) * unit


def inner_tables(rows_dev):
    freqs = rows_dev + 1
    fp = padded(freqs)
    f = np.arange(freqs)[:, None]
    n = np.arange(rows_dev)[None, :]
    phase = ((f * n) % (2 * rows_dev)) * (np.pi / rows_dev)
    fwd = np.zeros((2 * fp, rows_dev))
    fwd[:freqs] = np.cos(phase)
    fwd[fp : fp + freqs] = -np.sin(phase)
    t = np.arange(rows_dev)[:, None] + rows_dev
    f2 = np.arange(freqs)[None, :]
    phase2 = ((f2 * t) % (2 * rows_dev)) * (np.pi / rows_dev)
    weight = np.where((f2 == 0) | (f2 == rows_dev), 1.0, 2.0) / (2 * rows_dev)
    inv = np.zeros((rows_dev, 2 * fp))
    inv[:, :freqs] = weight * np.cos(phase2)
    inv[:, fp : fp + freqs] = -weight * np.sin(phase2)
    return fp, fwd, inv


def outer_tables(blocks, fp):
    size = 2 * blocks
    j = np.arange(blocks)[:, None]
    m = np.arange(size)[None, :]
    phase = 2 * np.pi * ((j * m) % size) / size
    fwd = np.concatenate([np.cos(phase), np.sin(phase)], axis=1)
    mi = np.arange(size)[:, None]
    i = np.arange(blocks)[None, :]
    phase_i = 2 * np.pi * ((mi * i) % size) / size
    cos_i = np.cos(phase_i) / size
    sin_i = np.sin(phase_i) / size
    inv_re = np.concatenate([cos_i, -sin_i], axis=0)
    inv_im = np.concatenate([sin_i, cos_i], axis=0)
    sign = np.where(np.arange(fp) % 2 == 0, 1.0, -1.0)[:, None]
    step = 2 * np.pi * np.arange(size)[None, :] / size
    shift_re = np.cos(step) + sign
    shift_im = -np.sin(step) + 0.0 * sign
    return fwd, inv_re, inv_im, shift_re, shift_im


def on_device(inputs, gate_values, causal_filter, anti_filter, skip_gain, norm_gain):
    rows_dev, chan_dev = inputs.shape
    blocks = lax.axis_size("seq")
    per = chan_dev // blocks
    size = 2 * blocks
    f32 = jnp.float32
    own_index = lax.axis_index("seq")

    fp, fwd_np, inv_np = inner_tables(rows_dev)
    ofwd_np, oinv_re_np, oinv_im_np, sh_re_np, sh_im_np = outer_tables(blocks, fp)
    fwd = jnp.asarray(fwd_np, jnp.bfloat16)
    inv = jnp.asarray(inv_np, f32)
    ofwd = jnp.asarray(ofwd_np, f32)
    oinv_re = jnp.asarray(oinv_re_np, f32)
    oinv_im = jnp.asarray(oinv_im_np, f32)
    sh_re = jnp.asarray(sh_re_np, f32)
    sh_im = jnp.asarray(sh_im_np, f32)

    stacked = jnp.stack([inputs, causal_filter, anti_filter, gate_values])
    lanes = 128
    eye_ch = jnp.eye(chan_dev, dtype=jnp.bfloat16)
    by_channel = jnp.einsum(
        "ck,atk->cat", eye_ch, stacked, preferred_element_type=f32
    ).astype(jnp.bfloat16)
    send = by_channel.reshape(blocks, per * 4 * rows_dev // lanes, lanes)
    recv = lax.all_to_all(send, "seq", 0, 0, tiled=True)
    series = recv.reshape(blocks, per, 4, rows_dev).transpose(0, 2, 1, 3)
    block_ids = lax.broadcasted_iota(jnp.int32, (blocks, 1, rows_dev), 0)
    tok_ids = lax.broadcasted_iota(jnp.int32, (blocks, 1, rows_dev), 2)
    first_row = jnp.logical_and(block_ids == 0, tok_ids == 0)
    anti_rows = jnp.where(first_row, jnp.zeros_like(series[:, 2]), series[:, 2])
    conv_in = jnp.stack([series[:, 0], series[:, 1], anti_rows], axis=1)
    conv_in = conv_in.reshape(blocks, 3 * per, rows_dev).transpose(1, 0, 2)

    spec = jnp.einsum("fn,qbn->qfb", fwd, conv_in, preferred_element_type=f32)
    spec = spec.astype(jnp.bfloat16).astype(f32)
    z = jnp.einsum("qfb,bk->qfk", spec, ofwd, precision=HIGHEST, preferred_element_type=f32)
    z_re, z_im = z[:, :fp], z[:, fp:]
    x_re = (z_re[..., :size] + z_im[..., size:]).reshape(3, per, fp, size)
    x_im = (z_im[..., :size] - z_re[..., size:]).reshape(3, per, fp, size)

    c_re = sh_re * x_re[1] - sh_im * x_im[1]
    c_im = sh_re * x_im[1] + sh_im * x_re[1]
    a_re = sh_re * x_re[2] - sh_im * x_im[2]
    a_im = sh_re * x_im[2] + sh_im * x_re[2]
    k_re = c_re + a_re
    k_im = c_im - a_im
    y_re = k_re * x_re[0] - k_im * x_im[0]
    y_im = k_re * x_im[0] + k_im * x_re[0]
    y_cat = jnp.concatenate([y_re, y_im], axis=-1)

    t_re = jnp.einsum("cfk,ki->cfi", y_cat, oinv_re, precision=HIGHEST, preferred_element_type=f32)
    t_im = jnp.einsum("cfk,ki->cfi", y_cat, oinv_im, precision=HIGHEST, preferred_element_type=f32)
    total = jnp.concatenate([t_re, t_im], axis=1)
    conv_t = jnp.einsum("cfi,tf->ict", total, inv, precision=HIGHEST, preferred_element_type=f32)

    skip_here = lax.dynamic_slice_in_dim(skip_gain, own_index * per, per)
    mixed_local = series[:, 3].astype(f32) * (
        conv_t + skip_here[None, :, None] * series[:, 0].astype(f32)
    )
    back = mixed_local.reshape(blocks, per * rows_dev // lanes, lanes)
    got = lax.all_to_all(back, "seq", 0, 0, tiled=True)
    mix_t = got.reshape(blocks * per, rows_dev)

    partial = jnp.sum(mix_t * mix_t, axis=0)
    squares = jnp.sum(lax.all_gather(partial, "ch", axis=0, tiled=False), axis=0)
    inv_norm = lax.rsqrt(squares / D + 1e-06)
    out_t = (norm_gain[:, None] * mix_t * inv_norm[None, :]).astype(jnp.bfloat16)
    eye_tok = jnp.eye(rows_dev, dtype=jnp.bfloat16)
    return jnp.einsum("tk,ck->tc", eye_tok, out_t, preferred_element_type=f32).astype(
        jnp.bfloat16
    )


def solution(mesh):
    placed = (P("seq", "ch"), P("seq", "ch"), P("seq", "ch"), P("seq", "ch"), P("ch"), P("ch"))
    return jax.shard_map(
        on_device, mesh=mesh, in_specs=placed, out_specs=P("seq", "ch"), check_vma=False
    )
```

```python
import numpy as np

import jax
import jax.numpy as jnp
from jax import lax
from jax.sharding import PartitionSpec as P

D = 1024
HIGHEST = lax.Precision.HIGHEST
HIGH = lax.Precision.HIGH


def padded(count, unit=8):
    return -(-count // unit) * unit


def inner_tables(rows_dev):
    freqs = rows_dev + 1
    fp = padded(freqs)
    f = np.arange(freqs)[:, None]
    n = np.arange(rows_dev)[None, :]
    phase = ((f * n) % (2 * rows_dev)) * (np.pi / rows_dev)
    fwd = np.zeros((2 * fp, rows_dev))
    fwd[:freqs] = np.cos(phase)
    fwd[fp : fp + freqs] = -np.sin(phase)
    t = np.arange(rows_dev)[:, None] + rows_dev
    f2 = np.arange(freqs)[None, :]
    phase2 = ((f2 * t) % (2 * rows_dev)) * (np.pi / rows_dev)
    weight = np.where((f2 == 0) | (f2 == rows_dev), 1.0, 2.0) / (2 * rows_dev)
    inv = np.zeros((rows_dev, 2 * fp))
    inv[:, :freqs] = weight * np.cos(phase2)
    inv[:, fp : fp + freqs] = -weight * np.sin(phase2)
    return fp, fwd, inv


def outer_tables(blocks, fp):
    size = 2 * blocks
    j = np.arange(blocks)[:, None]
    m = np.arange(size)[None, :]
    phase = 2 * np.pi * ((j * m) % size) / size
    fwd = np.concatenate([np.cos(phase), np.sin(phase)], axis=1)
    mi = np.arange(size)[:, None]
    i = np.arange(blocks)[None, :]
    phase_i = 2 * np.pi * ((mi * i) % size) / size
    cos_i = np.cos(phase_i) / size
    sin_i = np.sin(phase_i) / size
    inv_re = np.concatenate([cos_i, -sin_i], axis=0)
    inv_im = np.concatenate([sin_i, cos_i], axis=0)
    sign = np.where(np.arange(fp) % 2 == 0, 1.0, -1.0)[:, None]
    step = 2 * np.pi * np.arange(size)[None, :] / size
    return fwd, inv_re, inv_im, sign, np.cos(step), -np.sin(step)


def on_device(inputs, gate_values, causal_filter, anti_filter, skip_gain, norm_gain):
    rows_dev, chan_dev = inputs.shape
    blocks = lax.axis_size("seq")
    per = chan_dev // blocks
    size = 2 * blocks
    f32 = jnp.float32
    own_index = lax.axis_index("seq")

    fp, fwd_np, inv_np = inner_tables(rows_dev)
    ofwd_np, oinv_re_np, oinv_im_np, sign_np, cos_np, msin_np = outer_tables(blocks, fp)
    fwd = jnp.asarray(fwd_np, jnp.bfloat16)
    inv = jnp.asarray(inv_np, f32)
    ofwd = jnp.asarray(ofwd_np, f32)
    oinv_re = jnp.asarray(oinv_re_np, f32)
    oinv_im = jnp.asarray(oinv_im_np, f32)
    sh_re = jnp.asarray(sign_np, f32) + jnp.asarray(cos_np, f32)
    sh_im = jnp.asarray(msin_np, f32)

    stacked = jnp.stack([inputs, causal_filter, anti_filter, gate_values])
    lanes = 128
    eye_ch = jnp.eye(chan_dev, dtype=jnp.bfloat16)
    by_channel = jnp.einsum(
        "ck,atk->cat", eye_ch, stacked, preferred_element_type=f32
    ).astype(jnp.bfloat16)
    send = by_channel.reshape(blocks, per * 4 * rows_dev // lanes, lanes)
    recv = lax.all_to_all(send, "seq", 0, 0, tiled=True)
    series = recv.reshape(blocks, per, 4, rows_dev).transpose(0, 2, 1, 3)
    block_ids = lax.broadcasted_iota(jnp.int32, (blocks, 1, rows_dev), 0)
    tok_ids = lax.broadcasted_iota(jnp.int32, (blocks, 1, rows_dev), 2)
    first_row = jnp.logical_and(block_ids == 0, tok_ids == 0)
    anti_rows = jnp.where(first_row, jnp.zeros_like(series[:, 2]), series[:, 2])
    conv_in = jnp.stack([series[:, 0], series[:, 1], anti_rows], axis=1)
    conv_in = conv_in.reshape(blocks, 3 * per, rows_dev).transpose(1, 0, 2)

    spec = jnp.einsum("fn,qbn->qfb", fwd, conv_in, preferred_element_type=f32)
    spec = spec.astype(jnp.bfloat16).astype(f32)
    z = jnp.einsum("qfb,bk->qfk", spec, ofwd, precision=HIGH, preferred_element_type=f32)
    z_re, z_im = z[:, :fp], z[:, fp:]
    x_re = (z_re[..., :size] + z_im[..., size:]).reshape(3, per, fp, size)
    x_im = (z_im[..., :size] - z_re[..., size:]).reshape(3, per, fp, size)

    c_re = sh_re * x_re[1] - sh_im * x_im[1]
    c_im = sh_re * x_im[1] + sh_im * x_re[1]
    a_re = sh_re * x_re[2] - sh_im * x_im[2]
    a_im = sh_re * x_im[2] + sh_im * x_re[2]
    k_re = c_re + a_re
    k_im = c_im - a_im
    y_re = k_re * x_re[0] - k_im * x_im[0]
    y_im = k_re * x_im[0] + k_im * x_re[0]
    y_cat = jnp.concatenate([y_re, y_im], axis=-1)

    t_re = jnp.einsum("cfk,ki->cfi", y_cat, oinv_re, precision=HIGH, preferred_element_type=f32)
    t_im = jnp.einsum("cfk,ki->cfi", y_cat, oinv_im, precision=HIGH, preferred_element_type=f32)
    total = jnp.concatenate([t_re, t_im], axis=1)
    conv_t = jnp.einsum("cfi,tf->ict", total, inv, precision=HIGH, preferred_element_type=f32)

    skip_here = lax.dynamic_slice_in_dim(skip_gain, own_index * per, per)
    mixed_local = series[:, 3].astype(f32) * (
        conv_t + skip_here[None, :, None] * series[:, 0].astype(f32)
    )
    back = mixed_local.reshape(blocks, per * rows_dev // lanes, lanes)
    got = lax.all_to_all(back, "seq", 0, 0, tiled=True)
    mix_t = got.reshape(blocks * per, rows_dev)

    partial = jnp.sum(mix_t * mix_t, axis=0)
    squares = jnp.sum(lax.all_gather(partial, "ch", axis=0, tiled=False), axis=0)
    inv_norm = lax.rsqrt(squares / D + 1e-06)
    out_t = (norm_gain[:, None] * mix_t * inv_norm[None, :]).astype(jnp.bfloat16)
    eye_tok = jnp.eye(rows_dev, dtype=jnp.bfloat16)
    return jnp.einsum("tk,ck->tc", eye_tok, out_t, preferred_element_type=f32).astype(
        jnp.bfloat16
    )


def solution(mesh):
    placed = (P("seq", "ch"), P("seq", "ch"), P("seq", "ch"), P("seq", "ch"), P("ch"), P("ch"))
    return jax.shard_map(
        on_device, mesh=mesh, in_specs=placed, out_specs=P("seq", "ch"), check_vma=False
    )
```

```python
import numpy as np

import jax
import jax.numpy as jnp
from jax import lax
from jax.sharding import PartitionSpec as P

D = 1024
HIGHEST = lax.Precision.HIGHEST
HIGH = lax.Precision.HIGH


def padded(count, unit=8):
    return -(-count // unit) * unit


def inner_tables(rows_dev):
    freqs = rows_dev + 1
    fp = padded(freqs)
    f = np.arange(freqs)[:, None]
    n = np.arange(rows_dev)[None, :]
    phase = ((f * n) % (2 * rows_dev)) * (np.pi / rows_dev)
    fwd = np.zeros((2 * fp, rows_dev))
    fwd[:freqs] = np.cos(phase)
    fwd[fp : fp + freqs] = -np.sin(phase)
    t = np.arange(rows_dev)[:, None] + rows_dev
    f2 = np.arange(freqs)[None, :]
    phase2 = ((f2 * t) % (2 * rows_dev)) * (np.pi / rows_dev)
    weight = np.where((f2 == 0) | (f2 == rows_dev), 1.0, 2.0) / (2 * rows_dev)
    inv = np.zeros((rows_dev, 2 * fp))
    inv[:, :freqs] = weight * np.cos(phase2)
    inv[:, fp : fp + freqs] = -weight * np.sin(phase2)
    return fp, fwd, inv


def outer_tables(blocks, fp):
    size = 2 * blocks
    j = np.arange(blocks)[:, None]
    m = np.arange(size)[None, :]
    phase = 2 * np.pi * ((j * m) % size) / size
    fwd = np.concatenate([np.cos(phase), np.sin(phase)], axis=1)
    mi = np.arange(size)[:, None]
    i = np.arange(blocks)[None, :]
    phase_i = 2 * np.pi * ((mi * i) % size) / size
    cos_i = np.cos(phase_i) / size
    sin_i = np.sin(phase_i) / size
    inv_re = np.concatenate([cos_i, -sin_i], axis=0)
    inv_im = np.concatenate([sin_i, cos_i], axis=0)
    sign = np.where(np.arange(fp) % 2 == 0, 1.0, -1.0)[:, None]
    step = 2 * np.pi * np.arange(size)[None, :] / size
    return fwd, inv_re, inv_im, sign, np.cos(step), -np.sin(step)


def on_device(inputs, gate_values, causal_filter, anti_filter, skip_gain, norm_gain):
    rows_dev, chan_dev = inputs.shape
    blocks = lax.axis_size("seq")
    per = chan_dev // blocks
    size = 2 * blocks
    f32 = jnp.float32
    own_index = lax.axis_index("seq")

    fp, fwd_np, inv_np = inner_tables(rows_dev)
    ofwd_np, oinv_re_np, oinv_im_np, sign_np, cos_np, msin_np = outer_tables(blocks, fp)
    fwd = jnp.asarray(fwd_np, jnp.bfloat16)
    inv = jnp.asarray(inv_np, f32)
    ofwd = jnp.asarray(ofwd_np, f32)
    oinv_re = jnp.asarray(oinv_re_np, f32)
    oinv_im = jnp.asarray(oinv_im_np, f32)
    sh_re = jnp.asarray(sign_np, f32) + jnp.asarray(cos_np, f32)
    sh_im = jnp.asarray(msin_np, f32)

    stacked = jnp.stack([inputs, causal_filter, anti_filter, gate_values])
    lanes = 128
    eye_ch = jnp.eye(chan_dev, dtype=jnp.bfloat16)
    by_channel = jnp.einsum(
        "ck,atk->cat", eye_ch, stacked, preferred_element_type=f32
    ).astype(jnp.bfloat16)
    send = by_channel.reshape(blocks, per * 4 * rows_dev // lanes, lanes)
    recv = lax.all_to_all(send, "seq", 0, 0, tiled=True)
    series = recv.reshape(blocks, per, 4, rows_dev).transpose(0, 2, 1, 3)
    block_ids = lax.broadcasted_iota(jnp.int32, (blocks, 1, rows_dev), 0)
    tok_ids = lax.broadcasted_iota(jnp.int32, (blocks, 1, rows_dev), 2)
    first_row = jnp.logical_and(block_ids == 0, tok_ids == 0)
    anti_rows = jnp.where(first_row, jnp.zeros_like(series[:, 2]), series[:, 2])
    conv_in = jnp.stack([series[:, 0], series[:, 1], anti_rows], axis=1)
    conv_in = conv_in.reshape(blocks, 3 * per, rows_dev).transpose(1, 0, 2)

    spec = jnp.einsum("fn,qbn->qfb", fwd, conv_in, preferred_element_type=f32)
    spec = spec.astype(jnp.bfloat16).astype(f32)
    z = jnp.einsum("qfb,bk->qfk", spec, ofwd, precision=HIGH, preferred_element_type=f32)
    z_re, z_im = z[:, :fp], z[:, fp:]
    x_re = (z_re[..., :size] + z_im[..., size:]).reshape(3, per, fp, size)
    x_im = (z_im[..., :size] - z_re[..., size:]).reshape(3, per, fp, size)

    c_re = sh_re * x_re[1] - sh_im * x_im[1]
    c_im = sh_re * x_im[1] + sh_im * x_re[1]
    a_re = sh_re * x_re[2] - sh_im * x_im[2]
    a_im = sh_re * x_im[2] + sh_im * x_re[2]
    k_re = c_re + a_re
    k_im = c_im - a_im
    y_re = k_re * x_re[0] - k_im * x_im[0]
    y_im = k_re * x_im[0] + k_im * x_re[0]
    y_cat = jnp.concatenate([y_re, y_im], axis=-1)

    t_re = jnp.einsum("cfk,ki->cfi", y_cat, oinv_re, precision=HIGH, preferred_element_type=f32)
    t_im = jnp.einsum("cfk,ki->cfi", y_cat, oinv_im, precision=HIGH, preferred_element_type=f32)
    total = jnp.concatenate([t_re, t_im], axis=1)
    conv_t = jnp.einsum("cfi,tf->ict", total, inv, precision=HIGH, preferred_element_type=f32)

    skip_here = lax.dynamic_slice_in_dim(skip_gain, own_index * per, per)
    mixed_local = series[:, 3].astype(f32) * (
        conv_t + skip_here[None, :, None] * series[:, 0].astype(f32)
    )
    back = mixed_local.astype(jnp.bfloat16).reshape(blocks, per * rows_dev // lanes, lanes)
    got = lax.all_to_all(back, "seq", 0, 0, tiled=True)
    mix_t = got.reshape(blocks * per, rows_dev).astype(f32)

    partial = jnp.sum(mix_t * mix_t, axis=0)
    squares = jnp.sum(lax.all_gather(partial, "ch", axis=0, tiled=False), axis=0)
    inv_norm = lax.rsqrt(squares / D + 1e-06)
    out_t = (norm_gain[:, None] * mix_t * inv_norm[None, :]).astype(jnp.bfloat16)
    eye_tok = jnp.eye(rows_dev, dtype=jnp.bfloat16)
    return jnp.einsum("tk,ck->tc", eye_tok, out_t, preferred_element_type=f32).astype(
        jnp.bfloat16
    )


def solution(mesh):
    placed = (P("seq", "ch"), P("seq", "ch"), P("seq", "ch"), P("seq", "ch"), P("ch"), P("ch"))
    return jax.shard_map(
        on_device, mesh=mesh, in_specs=placed, out_specs=P("seq", "ch"), check_vma=False
    )
```

```python
import numpy as np

import jax
import jax.numpy as jnp
from jax import lax
from jax.sharding import PartitionSpec as P

D = 1024
HIGHEST = lax.Precision.HIGHEST
HIGH = lax.Precision.HIGH


def padded(count, unit=8):
    return -(-count // unit) * unit


def inner_tables(rows_dev):
    freqs = rows_dev + 1
    fp = padded(freqs)
    f = np.arange(freqs)[:, None]
    n = np.arange(rows_dev)[None, :]
    phase = ((f * n) % (2 * rows_dev)) * (np.pi / rows_dev)
    fwd = np.zeros((2 * fp, rows_dev))
    fwd[:freqs] = np.cos(phase)
    fwd[fp : fp + freqs] = -np.sin(phase)
    t = np.arange(rows_dev)[:, None] + rows_dev
    f2 = np.arange(freqs)[None, :]
    phase2 = ((f2 * t) % (2 * rows_dev)) * (np.pi / rows_dev)
    weight = np.where((f2 == 0) | (f2 == rows_dev), 1.0, 2.0) / (2 * rows_dev)
    inv = np.zeros((rows_dev, 2 * fp))
    inv[:, :freqs] = weight * np.cos(phase2)
    inv[:, fp : fp + freqs] = -weight * np.sin(phase2)
    return fp, fwd, inv


def outer_tables(blocks, fp):
    size = 2 * blocks
    j = np.arange(blocks)[:, None]
    m = np.arange(size)[None, :]
    phase = 2 * np.pi * ((j * m) % size) / size
    fwd = np.concatenate([np.cos(phase), np.sin(phase)], axis=1)
    mi = np.arange(size)[:, None]
    i = np.arange(blocks)[None, :]
    phase_i = 2 * np.pi * ((mi * i) % size) / size
    cos_i = np.cos(phase_i) / size
    sin_i = np.sin(phase_i) / size
    inv_re = np.concatenate([cos_i, -sin_i], axis=0)
    inv_im = np.concatenate([sin_i, cos_i], axis=0)
    sign = np.where(np.arange(fp) % 2 == 0, 1.0, -1.0)[:, None]
    step = 2 * np.pi * np.arange(size)[None, :] / size
    return fwd, inv_re, inv_im, sign, np.cos(step), -np.sin(step)


def on_device(inputs, gate_values, causal_filter, anti_filter, skip_gain, norm_gain):
    rows_dev, chan_dev = inputs.shape
    blocks = lax.axis_size("seq")
    per = chan_dev // blocks
    size = 2 * blocks
    f32 = jnp.float32
    own_index = lax.axis_index("seq")

    fp, fwd_np, inv_np = inner_tables(rows_dev)
    ofwd_np, oinv_re_np, oinv_im_np, sign_np, cos_np, msin_np = outer_tables(blocks, fp)
    fwd = jnp.asarray(fwd_np, jnp.bfloat16)
    inv = jnp.asarray(inv_np, f32)
    ofwd = jnp.asarray(ofwd_np, f32)
    oinv_re = jnp.asarray(oinv_re_np, f32)
    oinv_im = jnp.asarray(oinv_im_np, f32)
    sh_re = jnp.asarray(sign_np, f32) + jnp.asarray(cos_np, f32)
    sh_im = jnp.asarray(msin_np, f32)

    stacked = jnp.stack([inputs, causal_filter, anti_filter])
    lanes = 128
    eye_ch = jnp.eye(chan_dev, dtype=jnp.bfloat16)
    by_channel = jnp.einsum(
        "ck,atk->cat", eye_ch, stacked, preferred_element_type=f32
    ).astype(jnp.bfloat16)
    send = by_channel.reshape(blocks, per * 3 * rows_dev // lanes, lanes)
    recv = lax.all_to_all(send, "seq", 0, 0, tiled=True)
    series = recv.reshape(blocks, per, 3, rows_dev).transpose(0, 2, 1, 3)
    block_ids = lax.broadcasted_iota(jnp.int32, (blocks, 1, rows_dev), 0)
    tok_ids = lax.broadcasted_iota(jnp.int32, (blocks, 1, rows_dev), 2)
    first_row = jnp.logical_and(block_ids == 0, tok_ids == 0)
    anti_rows = jnp.where(first_row, jnp.zeros_like(series[:, 2]), series[:, 2])
    conv_in = jnp.stack([series[:, 0], series[:, 1], anti_rows], axis=1)
    conv_in = conv_in.reshape(blocks, 3 * per, rows_dev).transpose(1, 0, 2)

    spec = jnp.einsum("fn,qbn->qfb", fwd, conv_in, preferred_element_type=f32)
    spec = spec.astype(jnp.bfloat16).astype(f32)
    z = jnp.einsum("qfb,bk->qfk", spec, ofwd, precision=HIGH, preferred_element_type=f32)
    z_re, z_im = z[:, :fp], z[:, fp:]
    x_re = (z_re[..., :size] + z_im[..., size:]).reshape(3, per, fp, size)
    x_im = (z_im[..., :size] - z_re[..., size:]).reshape(3, per, fp, size)

    c_re = sh_re * x_re[1] - sh_im * x_im[1]
    c_im = sh_re * x_im[1] + sh_im * x_re[1]
    a_re = sh_re * x_re[2] - sh_im * x_im[2]
    a_im = sh_re * x_im[2] + sh_im * x_re[2]
    k_re = c_re + a_re
    k_im = c_im - a_im
    y_re = k_re * x_re[0] - k_im * x_im[0]
    y_im = k_re * x_im[0] + k_im * x_re[0]
    y_cat = jnp.concatenate([y_re, y_im], axis=-1)

    t_re = jnp.einsum("cfk,ki->cfi", y_cat, oinv_re, precision=HIGH, preferred_element_type=f32)
    t_im = jnp.einsum("cfk,ki->cfi", y_cat, oinv_im, precision=HIGH, preferred_element_type=f32)
    total = jnp.concatenate([t_re, t_im], axis=1)
    conv_t = jnp.einsum("cfi,tf->ict", total, inv, precision=HIGH, preferred_element_type=f32)

    back = conv_t.reshape(blocks, per * rows_dev // lanes, lanes)
    got = lax.all_to_all(back, "seq", 0, 0, tiled=True)
    conv_tc = got.reshape(blocks * per, rows_dev)
    eye_ch_f = jnp.eye(chan_dev, dtype=f32)
    gate_t = jnp.einsum("ck,tk->ct", eye_ch, gate_values, preferred_element_type=f32)
    inputs_t = jnp.einsum("ck,tk->ct", eye_ch, inputs, preferred_element_type=f32)
    mix_t = gate_t * (conv_tc + skip_gain[:, None] * inputs_t)

    partial = jnp.sum(mix_t * mix_t, axis=0)
    squares = jnp.sum(lax.all_gather(partial, "ch", axis=0, tiled=False), axis=0)
    inv_norm = lax.rsqrt(squares / D + 1e-06)
    out_t = (norm_gain[:, None] * mix_t * inv_norm[None, :]).astype(jnp.bfloat16)
    eye_tok = jnp.eye(rows_dev, dtype=jnp.bfloat16)
    return jnp.einsum("tk,ck->tc", eye_tok, out_t, preferred_element_type=f32).astype(
        jnp.bfloat16
    )


def solution(mesh):
    placed = (P("seq", "ch"), P("seq", "ch"), P("seq", "ch"), P("seq", "ch"), P("ch"), P("ch"))
    return jax.shard_map(
        on_device, mesh=mesh, in_specs=placed, out_specs=P("seq", "ch"), check_vma=False
    )
```

```python
import numpy as np

import jax
import jax.numpy as jnp
from jax import lax
from jax.sharding import PartitionSpec as P

D = 1024
HIGHEST = lax.Precision.HIGHEST
HIGH = lax.Precision.HIGH


def padded(count, unit=8):
    return -(-count // unit) * unit


def inner_tables(rows_dev):
    freqs = rows_dev + 1
    fp = padded(freqs)
    f = np.arange(freqs)[:, None]
    n = np.arange(rows_dev)[None, :]
    phase = ((f * n) % (2 * rows_dev)) * (np.pi / rows_dev)
    fwd = np.zeros((2 * fp, rows_dev))
    fwd[:freqs] = np.cos(phase)
    fwd[fp : fp + freqs] = -np.sin(phase)
    t = np.arange(rows_dev)[:, None] + rows_dev
    f2 = np.arange(freqs)[None, :]
    phase2 = ((f2 * t) % (2 * rows_dev)) * (np.pi / rows_dev)
    weight = np.where((f2 == 0) | (f2 == rows_dev), 1.0, 2.0) / (2 * rows_dev)
    inv = np.zeros((rows_dev, 2 * fp))
    inv[:, :freqs] = weight * np.cos(phase2)
    inv[:, fp : fp + freqs] = -weight * np.sin(phase2)
    return fp, fwd, inv


def outer_tables(blocks, fp):
    size = 2 * blocks
    j = np.arange(blocks)[:, None]
    m = np.arange(size)[None, :]
    phase = 2 * np.pi * ((j * m) % size) / size
    fwd = np.concatenate([np.cos(phase), np.sin(phase)], axis=1)
    mi = np.arange(size)[:, None]
    i = np.arange(blocks)[None, :]
    phase_i = 2 * np.pi * ((mi * i) % size) / size
    cos_i = np.cos(phase_i) / size
    sin_i = np.sin(phase_i) / size
    inv_re = np.concatenate([cos_i, -sin_i], axis=0)
    inv_im = np.concatenate([sin_i, cos_i], axis=0)
    sign = np.where(np.arange(fp) % 2 == 0, 1.0, -1.0)[:, None]
    step = 2 * np.pi * np.arange(size)[None, :] / size
    return fwd, inv_re, inv_im, sign, np.cos(step), -np.sin(step)


def on_device(inputs, gate_values, causal_filter, anti_filter, skip_gain, norm_gain):
    rows_dev, chan_dev = inputs.shape
    blocks = lax.axis_size("seq")
    per = chan_dev // blocks
    size = 2 * blocks
    f32 = jnp.float32
    own_index = lax.axis_index("seq")

    fp, fwd_np, inv_np = inner_tables(rows_dev)
    ofwd_np, oinv_re_np, oinv_im_np, sign_np, cos_np, msin_np = outer_tables(blocks, fp)
    fwd = jnp.asarray(fwd_np, jnp.bfloat16)
    inv = jnp.asarray(inv_np, f32)
    ofwd = jnp.asarray(ofwd_np, f32)
    oinv_re = jnp.asarray(oinv_re_np, f32)
    oinv_im = jnp.asarray(oinv_im_np, f32)
    sh_re = jnp.asarray(sign_np, f32) + jnp.asarray(cos_np, f32)
    sh_im = jnp.asarray(msin_np, f32)

    lanes = 128
    arrays = 4
    joined = jnp.concatenate([inputs, causal_filter, anti_filter, gate_values], axis=1)
    dest = np.arange(blocks)[:, None, None]
    kind = np.arange(arrays)[None, :, None]
    chan = np.arange(per)[None, None, :]
    source = (kind * chan_dev + dest * per + chan).reshape(-1)
    perm_np = np.zeros((arrays * chan_dev, arrays * chan_dev))
    perm_np[np.arange(arrays * chan_dev), source] = 1.0
    perm = jnp.asarray(perm_np, jnp.bfloat16)
    by_dest = jnp.einsum("rk,tk->rt", perm, joined, preferred_element_type=f32).astype(
        jnp.bfloat16
    )
    send = by_dest.reshape(blocks, arrays * per, rows_dev)
    recv = lax.all_to_all(send, "seq", 0, 0, tiled=True)
    series = recv.reshape(blocks, arrays, per, rows_dev)
    block_ids = lax.broadcasted_iota(jnp.int32, (blocks, 1, rows_dev), 0)
    tok_ids = lax.broadcasted_iota(jnp.int32, (blocks, 1, rows_dev), 2)
    first_row = jnp.logical_and(block_ids == 0, tok_ids == 0)
    anti_rows = jnp.where(first_row, jnp.zeros_like(series[:, 2]), series[:, 2])
    conv_in = jnp.stack([series[:, 0], series[:, 1], anti_rows], axis=1)
    conv_in = conv_in.reshape(blocks, 3 * per, rows_dev).transpose(1, 0, 2)

    spec = jnp.einsum("fn,qbn->qfb", fwd, conv_in, preferred_element_type=f32)
    spec = spec.astype(jnp.bfloat16).astype(f32)
    z = jnp.einsum("qfb,bk->qfk", spec, ofwd, precision=HIGH, preferred_element_type=f32)
    z_re, z_im = z[:, :fp], z[:, fp:]
    x_re = (z_re[..., :size] + z_im[..., size:]).reshape(3, per, fp, size)
    x_im = (z_im[..., :size] - z_re[..., size:]).reshape(3, per, fp, size)

    c_re = sh_re * x_re[1] - sh_im * x_im[1]
    c_im = sh_re * x_im[1] + sh_im * x_re[1]
    a_re = sh_re * x_re[2] - sh_im * x_im[2]
    a_im = sh_re * x_im[2] + sh_im * x_re[2]
    k_re = c_re + a_re
    k_im = c_im - a_im
    y_re = k_re * x_re[0] - k_im * x_im[0]
    y_im = k_re * x_im[0] + k_im * x_re[0]
    y_cat = jnp.concatenate([y_re, y_im], axis=-1)

    t_re = jnp.einsum("cfk,ki->cfi", y_cat, oinv_re, precision=HIGH, preferred_element_type=f32)
    t_im = jnp.einsum("cfk,ki->cfi", y_cat, oinv_im, precision=HIGH, preferred_element_type=f32)
    total = jnp.concatenate([t_re, t_im], axis=1)
    conv_t = jnp.einsum("cfi,tf->ict", total, inv, precision=HIGH, preferred_element_type=f32)

    skip_here = lax.dynamic_slice_in_dim(skip_gain, own_index * per, per)
    mixed_local = series[:, 3].astype(f32) * (
        conv_t + skip_here[None, :, None] * series[:, 0].astype(f32)
    )
    back = mixed_local.reshape(blocks, per * rows_dev // lanes, lanes)
    got = lax.all_to_all(back, "seq", 0, 0, tiled=True)
    mix_t = got.reshape(blocks * per, rows_dev)

    partial = jnp.sum(mix_t * mix_t, axis=0)
    squares = jnp.sum(lax.all_gather(partial, "ch", axis=0, tiled=False), axis=0)
    inv_norm = lax.rsqrt(squares / D + 1e-06)
    out_t = (norm_gain[:, None] * mix_t * inv_norm[None, :]).astype(jnp.bfloat16)
    eye_tok = jnp.eye(rows_dev, dtype=jnp.bfloat16)
    return jnp.einsum("tk,ck->tc", eye_tok, out_t, preferred_element_type=f32).astype(
        jnp.bfloat16
    )


def solution(mesh):
    placed = (P("seq", "ch"), P("seq", "ch"), P("seq", "ch"), P("seq", "ch"), P("ch"), P("ch"))
    return jax.shard_map(
        on_device, mesh=mesh, in_specs=placed, out_specs=P("seq", "ch"), check_vma=False
    )
```

```python
import numpy as np

import jax
import jax.numpy as jnp
from jax import lax
from jax.sharding import PartitionSpec as P

D = 1024
HIGHEST = lax.Precision.HIGHEST
HIGH = lax.Precision.HIGH


def padded(count, unit=8):
    return -(-count // unit) * unit


def inner_tables(rows_dev):
    freqs = rows_dev + 1
    fp = padded(freqs)
    f = np.arange(freqs)[:, None]
    n = np.arange(rows_dev)[None, :]
    phase = ((f * n) % (2 * rows_dev)) * (np.pi / rows_dev)
    fwd = np.zeros((2 * fp, rows_dev))
    fwd[:freqs] = np.cos(phase)
    fwd[fp : fp + freqs] = -np.sin(phase)
    t = np.arange(rows_dev)[:, None] + rows_dev
    f2 = np.arange(freqs)[None, :]
    phase2 = ((f2 * t) % (2 * rows_dev)) * (np.pi / rows_dev)
    weight = np.where((f2 == 0) | (f2 == rows_dev), 1.0, 2.0) / (2 * rows_dev)
    inv = np.zeros((rows_dev, 2 * fp))
    inv[:, :freqs] = weight * np.cos(phase2)
    inv[:, fp : fp + freqs] = -weight * np.sin(phase2)
    return fp, fwd, inv


def outer_tables(blocks, fp):
    size = 2 * blocks
    j = np.arange(blocks)[:, None]
    m = np.arange(size)[None, :]
    phase = 2 * np.pi * ((j * m) % size) / size
    fwd = np.concatenate([np.cos(phase), np.sin(phase)], axis=1)
    mi = np.arange(size)[:, None]
    i = np.arange(blocks)[None, :]
    phase_i = 2 * np.pi * ((mi * i) % size) / size
    cos_i = np.cos(phase_i) / size
    sin_i = np.sin(phase_i) / size
    inv_re = np.concatenate([cos_i, -sin_i], axis=0)
    inv_im = np.concatenate([sin_i, cos_i], axis=0)
    sign = np.where(np.arange(fp) % 2 == 0, 1.0, -1.0)[:, None]
    step = 2 * np.pi * np.arange(size)[None, :] / size
    return fwd, inv_re, inv_im, sign, np.cos(step), -np.sin(step)


def on_device(inputs, gate_values, causal_filter, anti_filter, skip_gain, norm_gain):
    rows_dev, chan_dev = inputs.shape
    blocks = lax.axis_size("seq")
    per = chan_dev // blocks
    size = 2 * blocks
    f32 = jnp.float32
    own_index = lax.axis_index("seq")

    fp, fwd_np, inv_np = inner_tables(rows_dev)
    ofwd_np, oinv_re_np, oinv_im_np, sign_np, cos_np, msin_np = outer_tables(blocks, fp)
    fwd = jnp.asarray(fwd_np, jnp.bfloat16)
    inv = jnp.asarray(inv_np, f32)
    ofwd_hi = ofwd_np.astype(np.float32).astype(jnp.bfloat16)
    ofwd_lo = (ofwd_np - ofwd_hi.astype(np.float64)).astype(np.float32).astype(jnp.bfloat16)
    ofwd_split = jnp.asarray(np.concatenate([ofwd_hi, ofwd_lo], axis=1), jnp.bfloat16)
    oinv_re = jnp.asarray(oinv_re_np, f32)
    oinv_im = jnp.asarray(oinv_im_np, f32)
    step = lax.broadcasted_iota(f32, (1, size), 1) * f32(2 * np.pi / size)
    step = step + f32(0.0) * own_index.astype(f32)
    sh_re = jnp.asarray(sign_np, f32) + jnp.cos(step)
    sh_im = -jnp.sin(step)

    stacked = jnp.stack([inputs, causal_filter, anti_filter, gate_values])
    lanes = 128
    eye_ch = jnp.eye(chan_dev, dtype=jnp.bfloat16)
    by_channel = jnp.einsum(
        "ck,atk->cat", eye_ch, stacked, preferred_element_type=f32
    ).astype(jnp.bfloat16)
    send = by_channel.reshape(blocks, per * 4 * rows_dev // lanes, lanes)
    recv = lax.all_to_all(send, "seq", 0, 0, tiled=True)
    series = recv.reshape(blocks, per, 4, rows_dev).transpose(0, 2, 1, 3)
    block_ids = lax.broadcasted_iota(jnp.int32, (blocks, 1, rows_dev), 0)
    tok_ids = lax.broadcasted_iota(jnp.int32, (blocks, 1, rows_dev), 2)
    first_row = jnp.logical_and(block_ids == 0, tok_ids == 0)
    anti_rows = jnp.where(first_row, jnp.zeros_like(series[:, 2]), series[:, 2])
    conv_in = jnp.stack([series[:, 0], series[:, 1], anti_rows], axis=1)
    conv_in = conv_in.reshape(blocks, 3 * per, rows_dev).transpose(1, 0, 2)

    spec = jnp.einsum("fn,qbn->qfb", fwd, conv_in, preferred_element_type=f32)
    spec = spec.astype(jnp.bfloat16)
    z_split = jnp.einsum("qfb,bk->qfk", spec, ofwd_split, preferred_element_type=f32)
    z = z_split[..., : 2 * size] + z_split[..., 2 * size :]
    z_re, z_im = z[:, :fp], z[:, fp:]
    x_re = (z_re[..., :size] + z_im[..., size:]).reshape(3, per, fp, size)
    x_im = (z_im[..., :size] - z_re[..., size:]).reshape(3, per, fp, size)

    c_re = sh_re * x_re[1] - sh_im * x_im[1]
    c_im = sh_re * x_im[1] + sh_im * x_re[1]
    a_re = sh_re * x_re[2] - sh_im * x_im[2]
    a_im = sh_re * x_im[2] + sh_im * x_re[2]
    k_re = c_re + a_re
    k_im = c_im - a_im
    y_re = k_re * x_re[0] - k_im * x_im[0]
    y_im = k_re * x_im[0] + k_im * x_re[0]
    y_cat = jnp.concatenate([y_re, y_im], axis=-1)

    t_re = jnp.einsum("cfk,ki->cfi", y_cat, oinv_re, precision=HIGH, preferred_element_type=f32)
    t_im = jnp.einsum("cfk,ki->cfi", y_cat, oinv_im, precision=HIGH, preferred_element_type=f32)
    total = jnp.concatenate([t_re, t_im], axis=1)
    conv_t = jnp.einsum("cfi,tf->ict", total, inv, precision=HIGH, preferred_element_type=f32)

    skip_here = lax.dynamic_slice_in_dim(skip_gain, own_index * per, per)
    mixed_local = series[:, 3].astype(f32) * (
        conv_t + skip_here[None, :, None] * series[:, 0].astype(f32)
    )
    back = mixed_local.reshape(blocks, per * rows_dev // lanes, lanes)
    got = lax.all_to_all(back, "seq", 0, 0, tiled=True)
    mix_t = got.reshape(blocks * per, rows_dev)

    partial = jnp.sum(mix_t * mix_t, axis=0)
    squares = jnp.sum(lax.all_gather(partial, "ch", axis=0, tiled=False), axis=0)
    inv_norm = lax.rsqrt(squares / D + 1e-06)
    out_t = (norm_gain[:, None] * mix_t * inv_norm[None, :]).astype(jnp.bfloat16)
    eye_tok = jnp.eye(rows_dev, dtype=jnp.bfloat16)
    return jnp.einsum("tk,ck->tc", eye_tok, out_t, preferred_element_type=f32).astype(
        jnp.bfloat16
    )


def solution(mesh):
    placed = (P("seq", "ch"), P("seq", "ch"), P("seq", "ch"), P("seq", "ch"), P("ch"), P("ch"))
    return jax.shard_map(
        on_device, mesh=mesh, in_specs=placed, out_specs=P("seq", "ch"), check_vma=False
    )
```

```python
import numpy as np

import jax
import jax.numpy as jnp
from jax import lax
from jax.sharding import PartitionSpec as P

D = 1024
HIGHEST = lax.Precision.HIGHEST
HIGH = lax.Precision.HIGH


def padded(count, unit=8):
    return -(-count // unit) * unit


def inner_tables(rows_dev):
    freqs = rows_dev + 1
    fp = padded(freqs)
    f = np.arange(freqs)[:, None]
    n = np.arange(rows_dev)[None, :]
    phase = ((f * n) % (2 * rows_dev)) * (np.pi / rows_dev)
    fwd = np.zeros((2 * fp, rows_dev))
    fwd[:freqs] = np.cos(phase)
    fwd[fp : fp + freqs] = -np.sin(phase)
    t = np.arange(rows_dev)[:, None] + rows_dev
    f2 = np.arange(freqs)[None, :]
    phase2 = ((f2 * t) % (2 * rows_dev)) * (np.pi / rows_dev)
    weight = np.where((f2 == 0) | (f2 == rows_dev), 1.0, 2.0) / (2 * rows_dev)
    inv = np.zeros((rows_dev, 2 * fp))
    inv[:, :freqs] = weight * np.cos(phase2)
    inv[:, fp : fp + freqs] = -weight * np.sin(phase2)
    return fp, fwd, inv


def outer_tables(blocks, fp):
    size = 2 * blocks
    j = np.arange(blocks)[:, None]
    m = np.arange(size)[None, :]
    phase = 2 * np.pi * ((j * m) % size) / size
    fwd = np.concatenate([np.cos(phase), np.sin(phase)], axis=1)
    mi = np.arange(size)[:, None]
    i = np.arange(blocks)[None, :]
    phase_i = 2 * np.pi * ((mi * i) % size) / size
    cos_i = np.cos(phase_i) / size
    sin_i = np.sin(phase_i) / size
    inv_re = np.concatenate([cos_i, -sin_i], axis=0)
    inv_im = np.concatenate([sin_i, cos_i], axis=0)
    sign = np.where(np.arange(fp) % 2 == 0, 1.0, -1.0)[:, None]
    step = 2 * np.pi * np.arange(size)[None, :] / size
    return fwd, inv_re, inv_im, sign, np.cos(step), -np.sin(step)


def on_device(inputs, gate_values, causal_filter, anti_filter, skip_gain, norm_gain):
    rows_dev, chan_dev = inputs.shape
    blocks = lax.axis_size("seq")
    per = chan_dev // blocks
    size = 2 * blocks
    f32 = jnp.float32
    own_index = lax.axis_index("seq")

    fp, fwd_np, inv_np = inner_tables(rows_dev)
    ofwd_np, oinv_re_np, oinv_im_np, sign_np, cos_np, msin_np = outer_tables(blocks, fp)
    fwd = jnp.asarray(fwd_np, jnp.bfloat16)
    inv = jnp.asarray(inv_np, f32)
    ofwd = jnp.asarray(ofwd_np, jnp.bfloat16)
    oinv = jnp.asarray(np.concatenate([oinv_re_np, oinv_im_np], axis=1), f32)
    sh_re = jnp.asarray(sign_np, f32) + jnp.asarray(cos_np, f32)
    sh_im = jnp.asarray(msin_np, f32)

    stacked = jnp.stack([inputs, causal_filter, anti_filter, gate_values])
    lanes = 128
    eye_ch = jnp.eye(chan_dev, dtype=jnp.bfloat16)
    by_channel = jnp.einsum(
        "ck,atk->cat", eye_ch, stacked, preferred_element_type=f32
    ).astype(jnp.bfloat16)
    send = by_channel.reshape(blocks, per * 4 * rows_dev // lanes, lanes)
    recv = lax.all_to_all(send, "seq", 0, 0, tiled=True)
    series = recv.reshape(blocks, per, 4, rows_dev).transpose(0, 2, 1, 3)
    block_ids = lax.broadcasted_iota(jnp.int32, (blocks, 1, rows_dev), 0)
    tok_ids = lax.broadcasted_iota(jnp.int32, (blocks, 1, rows_dev), 2)
    first_row = jnp.logical_and(block_ids == 0, tok_ids == 0)
    anti_rows = jnp.where(first_row, jnp.zeros_like(series[:, 2]), series[:, 2])
    conv_in = jnp.stack([series[:, 0], series[:, 1], anti_rows], axis=1)
    conv_in = conv_in.reshape(blocks, 3 * per, rows_dev).transpose(1, 0, 2)

    spec = jnp.einsum("fn,qbn->qfb", fwd, conv_in, preferred_element_type=f32)
    spec = spec.astype(jnp.bfloat16)
    z = jnp.einsum("qfb,bk->qfk", spec, ofwd, preferred_element_type=f32)
    z_re, z_im = z[:, :fp], z[:, fp:]
    x_re = (z_re[..., :size] + z_im[..., size:]).reshape(3, per, fp, size)
    x_im = (z_im[..., :size] - z_re[..., size:]).reshape(3, per, fp, size)

    c_re = sh_re * x_re[1] - sh_im * x_im[1]
    c_im = sh_re * x_im[1] + sh_im * x_re[1]
    a_re = sh_re * x_re[2] - sh_im * x_im[2]
    a_im = sh_re * x_im[2] + sh_im * x_re[2]
    k_re = c_re + a_re
    k_im = c_im - a_im
    y_re = k_re * x_re[0] - k_im * x_im[0]
    y_im = k_re * x_im[0] + k_im * x_re[0]
    y_cat = jnp.concatenate([y_re, y_im], axis=-1)

    t_both = jnp.einsum("cfk,ki->cfi", y_cat, oinv, precision=HIGH, preferred_element_type=f32)
    total = jnp.concatenate([t_both[..., :blocks], t_both[..., blocks:]], axis=1)
    conv_t = jnp.einsum("cfi,tf->ict", total, inv, precision=HIGH, preferred_element_type=f32)

    skip_here = lax.dynamic_slice_in_dim(skip_gain, own_index * per, per)
    mixed_local = series[:, 3].astype(f32) * (
        conv_t + skip_here[None, :, None] * series[:, 0].astype(f32)
    )
    back = mixed_local.reshape(blocks, per * rows_dev // lanes, lanes)
    got = lax.all_to_all(back, "seq", 0, 0, tiled=True)
    mix_t = got.reshape(blocks * per, rows_dev)

    partial = jnp.sum(mix_t * mix_t, axis=0)
    squares = jnp.sum(lax.all_gather(partial, "ch", axis=0, tiled=False), axis=0)
    inv_norm = lax.rsqrt(squares / D + 1e-06)
    out_t = (norm_gain[:, None] * mix_t * inv_norm[None, :]).astype(jnp.bfloat16)
    eye_tok = jnp.eye(rows_dev, dtype=jnp.bfloat16)
    return jnp.einsum("tk,ck->tc", eye_tok, out_t, preferred_element_type=f32).astype(
        jnp.bfloat16
    )


def solution(mesh):
    placed = (P("seq", "ch"), P("seq", "ch"), P("seq", "ch"), P("seq", "ch"), P("ch"), P("ch"))
    return jax.shard_map(
        on_device, mesh=mesh, in_specs=placed, out_specs=P("seq", "ch"), check_vma=False
    )
```

```python
import numpy as np

import jax
import jax.numpy as jnp
from jax import lax
from jax.sharding import PartitionSpec as P

D = 1024
HIGHEST = lax.Precision.HIGHEST
HIGH = lax.Precision.HIGH


def padded(count, unit=8):
    return -(-count // unit) * unit


def inner_tables(rows_dev):
    freqs = rows_dev + 1
    fp = padded(freqs)
    f = np.arange(freqs)[:, None]
    n = np.arange(rows_dev)[None, :]
    phase = ((f * n) % (2 * rows_dev)) * (np.pi / rows_dev)
    fwd = np.zeros((2 * fp, rows_dev))
    fwd[:freqs] = np.cos(phase)
    fwd[fp : fp + freqs] = -np.sin(phase)
    t = np.arange(rows_dev)[:, None] + rows_dev
    f2 = np.arange(freqs)[None, :]
    phase2 = ((f2 * t) % (2 * rows_dev)) * (np.pi / rows_dev)
    weight = np.where((f2 == 0) | (f2 == rows_dev), 1.0, 2.0) / (2 * rows_dev)
    inv = np.zeros((rows_dev, 2 * fp))
    inv[:, :freqs] = weight * np.cos(phase2)
    inv[:, fp : fp + freqs] = -weight * np.sin(phase2)
    return fp, fwd, inv


def outer_tables(blocks, fp):
    size = 2 * blocks
    j = np.arange(blocks)[:, None]
    m = np.arange(size)[None, :]
    phase = 2 * np.pi * ((j * m) % size) / size
    fwd = np.concatenate([np.cos(phase), np.sin(phase)], axis=1)
    mi = np.arange(size)[:, None]
    i = np.arange(blocks)[None, :]
    phase_i = 2 * np.pi * ((mi * i) % size) / size
    cos_i = np.cos(phase_i) / size
    sin_i = np.sin(phase_i) / size
    inv_re = np.concatenate([cos_i, -sin_i], axis=0)
    inv_im = np.concatenate([sin_i, cos_i], axis=0)
    sign = np.where(np.arange(fp) % 2 == 0, 1.0, -1.0)[:, None]
    step = 2 * np.pi * np.arange(size)[None, :] / size
    return fwd, inv_re, inv_im, sign, np.cos(step), -np.sin(step)


def on_device(inputs, gate_values, causal_filter, anti_filter, skip_gain, norm_gain):
    rows_dev, chan_dev = inputs.shape
    blocks = lax.axis_size("seq")
    per = chan_dev // blocks
    size = 2 * blocks
    f32 = jnp.float32
    own_index = lax.axis_index("seq")

    fp, fwd_np, inv_np = inner_tables(rows_dev)
    ofwd_np, oinv_re_np, oinv_im_np, sign_np, cos_np, msin_np = outer_tables(blocks, fp)
    fwd = jnp.asarray(fwd_np, jnp.bfloat16)
    inv = jnp.asarray(inv_np, f32)
    ofwd = jnp.asarray(ofwd_np, f32)
    oinv_re = jnp.asarray(oinv_re_np, f32)
    oinv_im = jnp.asarray(oinv_im_np, f32)
    sh_re = jnp.asarray(sign_np, f32) + jnp.asarray(cos_np, f32)
    sh_im = jnp.asarray(msin_np, f32)

    stacked = jnp.stack([inputs, causal_filter, anti_filter, gate_values])
    lanes = 128
    eye_ch = jnp.eye(chan_dev, dtype=jnp.bfloat16)
    by_channel = jnp.einsum(
        "ck,atk->cat", eye_ch, stacked, preferred_element_type=f32
    ).astype(jnp.bfloat16)
    send = by_channel.reshape(blocks, per * 4 * rows_dev // lanes, lanes)
    recv = lax.all_to_all(send, "seq", 0, 0, tiled=True)
    series = recv.reshape(blocks, per, 4, rows_dev).transpose(0, 2, 1, 3)
    block_ids = lax.broadcasted_iota(jnp.int32, (blocks, 1, rows_dev), 0)
    tok_ids = lax.broadcasted_iota(jnp.int32, (blocks, 1, rows_dev), 2)
    first_row = jnp.logical_and(block_ids == 0, tok_ids == 0)
    anti_rows = jnp.where(first_row, jnp.zeros_like(series[:, 2]), series[:, 2])
    conv_in = jnp.stack([series[:, 0], series[:, 1], anti_rows], axis=1)
    conv_in = conv_in.reshape(blocks, 3 * per, rows_dev).transpose(1, 0, 2)

    spec = jnp.einsum("fn,qbn->qfb", fwd, conv_in, preferred_element_type=f32)
    spec = spec.astype(jnp.bfloat16).astype(f32)
    z = jnp.einsum("qfb,bk->qfk", spec, ofwd, precision=HIGHEST, preferred_element_type=f32)
    z_re, z_im = z[:, :fp], z[:, fp:]
    x_re = (z_re[..., :size] + z_im[..., size:]).reshape(3, per, fp, size)
    x_im = (z_im[..., :size] - z_re[..., size:]).reshape(3, per, fp, size)

    c_re = sh_re * x_re[1] - sh_im * x_im[1]
    c_im = sh_re * x_im[1] + sh_im * x_re[1]
    a_re = sh_re * x_re[2] - sh_im * x_im[2]
    a_im = sh_re * x_im[2] + sh_im * x_re[2]
    k_re = c_re + a_re
    k_im = c_im - a_im
    y_re = k_re * x_re[0] - k_im * x_im[0]
    y_im = k_re * x_im[0] + k_im * x_re[0]
    y_cat = jnp.concatenate([y_re, y_im], axis=-1)

    t_re = jnp.einsum("cfk,ki->cfi", y_cat, oinv_re, precision=HIGHEST, preferred_element_type=f32)
    t_im = jnp.einsum("cfk,ki->cfi", y_cat, oinv_im, precision=HIGHEST, preferred_element_type=f32)
    total = jnp.concatenate([t_re, t_im], axis=1)
    conv_t = jnp.einsum("cfi,tf->ict", total, inv, precision=HIGH, preferred_element_type=f32)

    skip_here = lax.dynamic_slice_in_dim(skip_gain, own_index * per, per)
    mixed_local = series[:, 3].astype(f32) * (
        conv_t + skip_here[None, :, None] * series[:, 0].astype(f32)
    )
    back = mixed_local.reshape(blocks, per * rows_dev // lanes, lanes)
    got = lax.all_to_all(back, "seq", 0, 0, tiled=True)
    mix_t = got.reshape(blocks * per, rows_dev)

    partial = jnp.sum(mix_t * mix_t, axis=0)
    squares = jnp.sum(lax.all_gather(partial, "ch", axis=0, tiled=False), axis=0)
    inv_norm = lax.rsqrt(squares / D + 1e-06)
    out_t = (norm_gain[:, None] * mix_t * inv_norm[None, :]).astype(jnp.bfloat16)
    eye_tok = jnp.eye(rows_dev, dtype=jnp.bfloat16)
    return jnp.einsum("tk,ck->tc", eye_tok, out_t, preferred_element_type=f32).astype(
        jnp.bfloat16
    )


def solution(mesh):
    placed = (P("seq", "ch"), P("seq", "ch"), P("seq", "ch"), P("seq", "ch"), P("ch"), P("ch"))
    return jax.shard_map(
        on_device, mesh=mesh, in_specs=placed, out_specs=P("seq", "ch"), check_vma=False
    )
```

```python
import numpy as np

import jax
import jax.numpy as jnp
from jax import lax
from jax.sharding import PartitionSpec as P

D = 1024
HIGHEST = lax.Precision.HIGHEST
HIGH = lax.Precision.HIGH


def padded(count, unit=8):
    return -(-count // unit) * unit


def inner_tables(rows_dev):
    freqs = rows_dev + 1
    fp = padded(freqs)
    f = np.arange(freqs)[:, None]
    n = np.arange(rows_dev)[None, :]
    phase = ((f * n) % (2 * rows_dev)) * (np.pi / rows_dev)
    fwd = np.zeros((2 * fp, rows_dev))
    fwd[:freqs] = np.cos(phase)
    fwd[fp : fp + freqs] = -np.sin(phase)
    t = np.arange(rows_dev)[:, None] + rows_dev
    f2 = np.arange(freqs)[None, :]
    phase2 = ((f2 * t) % (2 * rows_dev)) * (np.pi / rows_dev)
    weight = np.where((f2 == 0) | (f2 == rows_dev), 1.0, 2.0) / (2 * rows_dev)
    inv = np.zeros((rows_dev, 2 * fp))
    inv[:, :freqs] = weight * np.cos(phase2)
    inv[:, fp : fp + freqs] = -weight * np.sin(phase2)
    return fp, fwd, inv


def outer_tables(blocks, fp):
    size = 2 * blocks
    j = np.arange(blocks)[:, None]
    m = np.arange(size)[None, :]
    phase = 2 * np.pi * ((j * m) % size) / size
    fwd = np.concatenate([np.cos(phase), np.sin(phase)], axis=1)
    mi = np.arange(size)[:, None]
    i = np.arange(blocks)[None, :]
    phase_i = 2 * np.pi * ((mi * i) % size) / size
    cos_i = np.cos(phase_i) / size
    sin_i = np.sin(phase_i) / size
    inv_re = np.concatenate([cos_i, -sin_i], axis=0)
    inv_im = np.concatenate([sin_i, cos_i], axis=0)
    sign = np.where(np.arange(fp) % 2 == 0, 1.0, -1.0)[:, None]
    step = 2 * np.pi * np.arange(size)[None, :] / size
    return fwd, inv_re, inv_im, sign, np.cos(step), -np.sin(step)


def on_device(inputs, gate_values, causal_filter, anti_filter, skip_gain, norm_gain):
    rows_dev, chan_dev = inputs.shape
    blocks = lax.axis_size("seq")
    per = chan_dev // blocks
    size = 2 * blocks
    f32 = jnp.float32
    own_index = lax.axis_index("seq")

    fp, fwd_np, inv_np = inner_tables(rows_dev)
    ofwd_np, oinv_re_np, oinv_im_np, sign_np, cos_np, msin_np = outer_tables(blocks, fp)
    fwd = jnp.asarray(fwd_np, jnp.bfloat16)
    inv = jnp.asarray(inv_np, f32)
    part_hi = ofwd_np.astype(np.float32).astype(jnp.bfloat16)
    rest = ofwd_np - part_hi.astype(np.float64)
    part_mid = rest.astype(np.float32).astype(jnp.bfloat16)
    part_lo = (rest - part_mid.astype(np.float64)).astype(np.float32).astype(jnp.bfloat16)
    ofwd_parts = [jnp.asarray(p, jnp.bfloat16) for p in (part_hi, part_mid, part_lo)]
    oinv_re = jnp.asarray(oinv_re_np, f32)
    oinv_im = jnp.asarray(oinv_im_np, f32)
    sh_re = jnp.asarray(sign_np, f32) + jnp.asarray(cos_np, f32)
    sh_im = jnp.asarray(msin_np, f32)

    stacked = jnp.stack([inputs, causal_filter, anti_filter, gate_values])
    lanes = 128
    eye_ch = jnp.eye(chan_dev, dtype=jnp.bfloat16)
    by_channel = jnp.einsum(
        "ck,atk->cat", eye_ch, stacked, preferred_element_type=f32
    ).astype(jnp.bfloat16)
    send = by_channel.reshape(blocks, per * 4 * rows_dev // lanes, lanes)
    recv = lax.all_to_all(send, "seq", 0, 0, tiled=True)
    series = recv.reshape(blocks, per, 4, rows_dev).transpose(0, 2, 1, 3)
    block_ids = lax.broadcasted_iota(jnp.int32, (blocks, 1, rows_dev), 0)
    tok_ids = lax.broadcasted_iota(jnp.int32, (blocks, 1, rows_dev), 2)
    first_row = jnp.logical_and(block_ids == 0, tok_ids == 0)
    anti_rows = jnp.where(first_row, jnp.zeros_like(series[:, 2]), series[:, 2])
    conv_in = jnp.stack([series[:, 0], series[:, 1], anti_rows], axis=1)
    conv_in = conv_in.reshape(blocks, 3 * per, rows_dev).transpose(1, 0, 2)

    spec = jnp.einsum("fn,qbn->qfb", fwd, conv_in, preferred_element_type=f32)
    spec = spec.astype(jnp.bfloat16)
    z_parts = [
        jnp.einsum("qfb,bk->qfk", spec, part, preferred_element_type=f32) for part in ofwd_parts
    ]
    z = z_parts[2] + z_parts[1] + z_parts[0]
    z_re, z_im = z[:, :fp], z[:, fp:]
    x_re = (z_re[..., :size] + z_im[..., size:]).reshape(3, per, fp, size)
    x_im = (z_im[..., :size] - z_re[..., size:]).reshape(3, per, fp, size)

    c_re = sh_re * x_re[1] - sh_im * x_im[1]
    c_im = sh_re * x_im[1] + sh_im * x_re[1]
    a_re = sh_re * x_re[2] - sh_im * x_im[2]
    a_im = sh_re * x_im[2] + sh_im * x_re[2]
    k_re = c_re + a_re
    k_im = c_im - a_im
    y_re = k_re * x_re[0] - k_im * x_im[0]
    y_im = k_re * x_im[0] + k_im * x_re[0]
    y_cat = jnp.concatenate([y_re, y_im], axis=-1)

    t_re = jnp.einsum("cfk,ki->cfi", y_cat, oinv_re, precision=HIGHEST, preferred_element_type=f32)
    t_im = jnp.einsum("cfk,ki->cfi", y_cat, oinv_im, precision=HIGHEST, preferred_element_type=f32)
    total = jnp.concatenate([t_re, t_im], axis=1)
    conv_t = jnp.einsum("cfi,tf->ict", total, inv, precision=HIGH, preferred_element_type=f32)

    skip_here = lax.dynamic_slice_in_dim(skip_gain, own_index * per, per)
    mixed_local = series[:, 3].astype(f32) * (
        conv_t + skip_here[None, :, None] * series[:, 0].astype(f32)
    )
    back = mixed_local.reshape(blocks, per * rows_dev // lanes, lanes)
    got = lax.all_to_all(back, "seq", 0, 0, tiled=True)
    mix_t = got.reshape(blocks * per, rows_dev)

    partial = jnp.sum(mix_t * mix_t, axis=0)
    squares = jnp.sum(lax.all_gather(partial, "ch", axis=0, tiled=False), axis=0)
    inv_norm = lax.rsqrt(squares / D + 1e-06)
    out_t = (norm_gain[:, None] * mix_t * inv_norm[None, :]).astype(jnp.bfloat16)
    eye_tok = jnp.eye(rows_dev, dtype=jnp.bfloat16)
    return jnp.einsum("tk,ck->tc", eye_tok, out_t, preferred_element_type=f32).astype(
        jnp.bfloat16
    )


def solution(mesh):
    placed = (P("seq", "ch"), P("seq", "ch"), P("seq", "ch"), P("seq", "ch"), P("ch"), P("ch"))
    return jax.shard_map(
        on_device, mesh=mesh, in_specs=placed, out_specs=P("seq", "ch"), check_vma=False
    )
```

```python
import numpy as np

import jax
import jax.numpy as jnp
from jax import lax
from jax.sharding import PartitionSpec as P

D = 1024
HIGHEST = lax.Precision.HIGHEST
HIGH = lax.Precision.HIGH


def padded(count, unit=8):
    return -(-count // unit) * unit


def inner_tables(rows_dev):
    freqs = rows_dev + 1
    fp = padded(freqs)
    f = np.arange(freqs)[:, None]
    n = np.arange(rows_dev)[None, :]
    phase = ((f * n) % (2 * rows_dev)) * (np.pi / rows_dev)
    fwd = np.zeros((2 * fp, rows_dev))
    fwd[:freqs] = np.cos(phase)
    fwd[fp : fp + freqs] = -np.sin(phase)
    t = np.arange(rows_dev)[:, None] + rows_dev
    f2 = np.arange(freqs)[None, :]
    phase2 = ((f2 * t) % (2 * rows_dev)) * (np.pi / rows_dev)
    weight = np.where((f2 == 0) | (f2 == rows_dev), 1.0, 2.0) / (2 * rows_dev)
    inv = np.zeros((rows_dev, 2 * fp))
    inv[:, :freqs] = weight * np.cos(phase2)
    inv[:, fp : fp + freqs] = -weight * np.sin(phase2)
    return fp, fwd, inv


def outer_tables(blocks, fp):
    size = 2 * blocks
    j = np.arange(blocks)[:, None]
    m = np.arange(size)[None, :]
    phase = 2 * np.pi * ((j * m) % size) / size
    fwd = np.concatenate([np.cos(phase), np.sin(phase)], axis=1)
    mi = np.arange(size)[:, None]
    i = np.arange(blocks)[None, :]
    phase_i = 2 * np.pi * ((mi * i) % size) / size
    cos_i = np.cos(phase_i) / size
    sin_i = np.sin(phase_i) / size
    inv_re = np.concatenate([cos_i, -sin_i], axis=0)
    inv_im = np.concatenate([sin_i, cos_i], axis=0)
    sign = np.where(np.arange(fp) % 2 == 0, 1.0, -1.0)[:, None]
    step = 2 * np.pi * np.arange(size)[None, :] / size
    return fwd, inv_re, inv_im, sign, np.cos(step), -np.sin(step)


def on_device(inputs, gate_values, causal_filter, anti_filter, skip_gain, norm_gain):
    rows_dev, chan_dev = inputs.shape
    blocks = lax.axis_size("seq")
    per = chan_dev // blocks
    size = 2 * blocks
    f32 = jnp.float32
    own_index = lax.axis_index("seq")

    fp, fwd_np, inv_np = inner_tables(rows_dev)
    ofwd_np, oinv_re_np, oinv_im_np, sign_np, cos_np, msin_np = outer_tables(blocks, fp)
    fwd = jnp.asarray(fwd_np, jnp.bfloat16)
    inv = jnp.asarray(inv_np, f32)
    ofwd = jnp.asarray(ofwd_np, f32)
    oinv = jnp.asarray(np.concatenate([oinv_re_np, oinv_im_np], axis=1), f32)
    sh_re = jnp.asarray(sign_np, f32) + jnp.asarray(cos_np, f32)
    sh_im = jnp.asarray(msin_np, f32)

    stacked = jnp.stack([inputs, causal_filter, anti_filter, gate_values])
    lanes = 128
    eye_ch = jnp.eye(chan_dev, dtype=jnp.bfloat16)
    by_channel = jnp.einsum(
        "ck,atk->cat", eye_ch, stacked, preferred_element_type=f32
    ).astype(jnp.bfloat16)
    send = by_channel.reshape(blocks, per * 4 * rows_dev // lanes, lanes)
    recv = lax.all_to_all(send, "seq", 0, 0, tiled=True)
    series = recv.reshape(blocks, per, 4, rows_dev).transpose(0, 2, 1, 3)
    block_ids = lax.broadcasted_iota(jnp.int32, (blocks, 1, rows_dev), 0)
    tok_ids = lax.broadcasted_iota(jnp.int32, (blocks, 1, rows_dev), 2)
    first_row = jnp.logical_and(block_ids == 0, tok_ids == 0)
    anti_rows = jnp.where(first_row, jnp.zeros_like(series[:, 2]), series[:, 2])
    conv_in = jnp.stack([series[:, 0], series[:, 1], anti_rows], axis=1)
    conv_in = conv_in.reshape(blocks, 3 * per, rows_dev).transpose(1, 0, 2)

    spec = jnp.einsum("fn,qbn->qfb", fwd, conv_in, preferred_element_type=f32)
    spec = spec.astype(jnp.bfloat16).astype(f32)
    z = jnp.einsum("qfb,bk->qfk", spec, ofwd, precision=HIGHEST, preferred_element_type=f32)
    z_re, z_im = z[:, :fp], z[:, fp:]
    x_re = (z_re[..., :size] + z_im[..., size:]).reshape(3, per, fp, size)
    x_im = (z_im[..., :size] - z_re[..., size:]).reshape(3, per, fp, size)

    c_re = sh_re * x_re[1] - sh_im * x_im[1]
    c_im = sh_re * x_im[1] + sh_im * x_re[1]
    a_re = sh_re * x_re[2] - sh_im * x_im[2]
    a_im = sh_re * x_im[2] + sh_im * x_re[2]
    k_re = c_re + a_re
    k_im = c_im - a_im
    y_re = k_re * x_re[0] - k_im * x_im[0]
    y_im = k_re * x_im[0] + k_im * x_re[0]
    y_cat = jnp.concatenate([y_re, y_im], axis=-1)

    t_both = jnp.einsum("cfk,ki->cfi", y_cat, oinv, precision=HIGHEST, preferred_element_type=f32)
    total = jnp.concatenate([t_both[..., :blocks], t_both[..., blocks:]], axis=1)
    conv_t = jnp.einsum("cfi,tf->ict", total, inv, precision=HIGH, preferred_element_type=f32)

    skip_here = lax.dynamic_slice_in_dim(skip_gain, own_index * per, per)
    mixed_local = series[:, 3].astype(f32) * (
        conv_t + skip_here[None, :, None] * series[:, 0].astype(f32)
    )
    back = mixed_local.reshape(blocks, per * rows_dev // lanes, lanes)
    got = lax.all_to_all(back, "seq", 0, 0, tiled=True)
    mix_t = got.reshape(blocks * per, rows_dev)

    partial = jnp.sum(mix_t * mix_t, axis=0)
    squares = jnp.sum(lax.all_gather(partial, "ch", axis=0, tiled=False), axis=0)
    inv_norm = lax.rsqrt(squares / D + 1e-06)
    out_t = (norm_gain[:, None] * mix_t * inv_norm[None, :]).astype(jnp.bfloat16)
    eye_tok = jnp.eye(rows_dev, dtype=jnp.bfloat16)
    return jnp.einsum("tk,ck->tc", eye_tok, out_t, preferred_element_type=f32).astype(
        jnp.bfloat16
    )


def solution(mesh):
    placed = (P("seq", "ch"), P("seq", "ch"), P("seq", "ch"), P("seq", "ch"), P("ch"), P("ch"))
    return jax.shard_map(
        on_device, mesh=mesh, in_specs=placed, out_specs=P("seq", "ch"), check_vma=False
    )
```

```python
import numpy as np

import jax
import jax.numpy as jnp
from jax import lax
from jax.sharding import PartitionSpec as P

D = 1024
HIGHEST = lax.Precision.HIGHEST
HIGH = lax.Precision.HIGH


def padded(count, unit=8):
    return -(-count // unit) * unit


def inner_tables(rows_dev):
    freqs = rows_dev + 1
    fp = padded(freqs)
    f = np.arange(freqs)[:, None]
    n = np.arange(rows_dev)[None, :]
    phase = ((f * n) % (2 * rows_dev)) * (np.pi / rows_dev)
    fwd = np.zeros((2 * fp, rows_dev))
    fwd[:freqs] = np.cos(phase)
    fwd[fp : fp + freqs] = -np.sin(phase)
    t = np.arange(rows_dev)[:, None] + rows_dev
    f2 = np.arange(freqs)[None, :]
    phase2 = ((f2 * t) % (2 * rows_dev)) * (np.pi / rows_dev)
    weight = np.where((f2 == 0) | (f2 == rows_dev), 1.0, 2.0) / (2 * rows_dev)
    inv = np.zeros((rows_dev, 2 * fp))
    inv[:, :freqs] = weight * np.cos(phase2)
    inv[:, fp : fp + freqs] = -weight * np.sin(phase2)
    return fp, fwd, inv


def outer_tables(blocks, fp):
    size = 2 * blocks
    j = np.arange(blocks)[:, None]
    m = np.arange(size)[None, :]
    phase = 2 * np.pi * ((j * m) % size) / size
    fwd = np.concatenate([np.cos(phase), np.sin(phase)], axis=1)
    phase1 = 2 * np.pi * (((j + 1) * m) % size) / size
    fwd_shift = np.concatenate([np.cos(phase1), np.sin(phase1)], axis=1)
    mi = np.arange(size)[:, None]
    i = np.arange(blocks)[None, :]
    phase_i = 2 * np.pi * ((mi * i) % size) / size
    cos_i = np.cos(phase_i) / size
    sin_i = np.sin(phase_i) / size
    inv_re = np.concatenate([cos_i, -sin_i], axis=0)
    inv_im = np.concatenate([sin_i, cos_i], axis=0)
    sign = np.where(np.arange(fp) % 2 == 0, 1.0, -1.0)[:, None]
    step = 2 * np.pi * np.arange(size)[None, :] / size
    return fwd, fwd_shift, inv_re, inv_im


def on_device(inputs, gate_values, causal_filter, anti_filter, skip_gain, norm_gain):
    rows_dev, chan_dev = inputs.shape
    blocks = lax.axis_size("seq")
    per = chan_dev // blocks
    size = 2 * blocks
    f32 = jnp.float32
    own_index = lax.axis_index("seq")

    fp, fwd_np, inv_np = inner_tables(rows_dev)
    ofwd_np, oshift_np, oinv_re_np, oinv_im_np = outer_tables(blocks, fp)
    fwd = jnp.asarray(fwd_np, jnp.bfloat16)
    inv = jnp.asarray(inv_np, f32)
    ofwd = jnp.asarray(ofwd_np, f32)
    oseg = jnp.asarray(np.concatenate([oshift_np, ofwd_np], axis=0), f32)
    oinv = jnp.asarray(np.concatenate([oinv_re_np, oinv_im_np], axis=1), f32)

    stacked = jnp.stack([inputs, causal_filter, anti_filter, gate_values])
    lanes = 128
    eye_ch = jnp.eye(chan_dev, dtype=jnp.bfloat16)
    by_channel = jnp.einsum(
        "ck,atk->cat", eye_ch, stacked, preferred_element_type=f32
    ).astype(jnp.bfloat16)
    send = by_channel.reshape(blocks, per * 4 * rows_dev // lanes, lanes)
    recv = lax.all_to_all(send, "seq", 0, 0, tiled=True)
    series = recv.reshape(blocks, per, 4, rows_dev).transpose(0, 2, 1, 3)
    block_ids = lax.broadcasted_iota(jnp.int32, (blocks, 1, rows_dev), 0)
    tok_ids = lax.broadcasted_iota(jnp.int32, (blocks, 1, rows_dev), 2)
    first_row = jnp.logical_and(block_ids == 0, tok_ids == 0)
    anti_rows = jnp.where(first_row, jnp.zeros_like(series[:, 2]), series[:, 2])
    conv_in = jnp.stack([series[:, 0], series[:, 1], anti_rows], axis=1)
    conv_in = conv_in.reshape(blocks, 3 * per, rows_dev).transpose(1, 0, 2)

    spec = jnp.einsum("fn,qbn->qfb", fwd, conv_in, preferred_element_type=f32)
    spec = spec.astype(jnp.bfloat16).astype(f32)
    spec = spec.reshape(3, per, 2 * fp, blocks)
    row_ids = lax.broadcasted_iota(jnp.int32, (2 * fp, 1), 0)
    sign = (1 - 2 * (row_ids % 2)).astype(f32)
    filt = spec[1:]
    seg_in = jnp.concatenate([filt, sign * filt], axis=-1)
    z_x = jnp.einsum("cfb,bk->cfk", spec[0], ofwd, precision=HIGHEST, preferred_element_type=f32)
    z_s = jnp.einsum("acfb,bk->acfk", seg_in, oseg, precision=HIGHEST, preferred_element_type=f32)

    def halves(z):
        z_re, z_im = z[..., :fp, :], z[..., fp:, :]
        return z_re[..., :size] + z_im[..., size:], z_im[..., :size] - z_re[..., size:]

    x_re, x_im = halves(z_x)
    s_re, s_im = halves(z_s)
    k_re = s_re[0] + s_re[1]
    k_im = s_im[0] - s_im[1]
    y_re = k_re * x_re - k_im * x_im
    y_im = k_re * x_im + k_im * x_re
    y_cat = jnp.concatenate([y_re, y_im], axis=-1)

    t_both = jnp.einsum("cfk,ki->cfi", y_cat, oinv, precision=HIGHEST, preferred_element_type=f32)
    total = jnp.concatenate([t_both[..., :blocks], t_both[..., blocks:]], axis=1)
    conv_t = jnp.einsum("cfi,tf->ict", total, inv, precision=HIGH, preferred_element_type=f32)

    skip_here = lax.dynamic_slice_in_dim(skip_gain, own_index * per, per)
    mixed_local = series[:, 3].astype(f32) * (
        conv_t + skip_here[None, :, None] * series[:, 0].astype(f32)
    )
    back = mixed_local.reshape(blocks, per * rows_dev // lanes, lanes)
    got = lax.all_to_all(back, "seq", 0, 0, tiled=True)
    mix_t = got.reshape(blocks * per, rows_dev)

    partial = jnp.sum(mix_t * mix_t, axis=0)
    squares = jnp.sum(lax.all_gather(partial, "ch", axis=0, tiled=False), axis=0)
    inv_norm = lax.rsqrt(squares / D + 1e-06)
    out_t = (norm_gain[:, None] * mix_t * inv_norm[None, :]).astype(jnp.bfloat16)
    eye_tok = jnp.eye(rows_dev, dtype=jnp.bfloat16)
    return jnp.einsum("tk,ck->tc", eye_tok, out_t, preferred_element_type=f32).astype(
        jnp.bfloat16
    )


def solution(mesh):
    placed = (P("seq", "ch"), P("seq", "ch"), P("seq", "ch"), P("seq", "ch"), P("ch"), P("ch"))
    return jax.shard_map(
        on_device, mesh=mesh, in_specs=placed, out_specs=P("seq", "ch"), check_vma=False
    )
```

```python
import numpy as np

import jax
import jax.numpy as jnp
from jax import lax
from jax.sharding import PartitionSpec as P

D = 1024
HIGHEST = lax.Precision.HIGHEST
HIGH = lax.Precision.HIGH


def padded(count, unit=8):
    return -(-count // unit) * unit


def inner_tables(rows_dev):
    freqs = rows_dev + 1
    fp = padded(freqs)
    f = np.arange(freqs)[:, None]
    n = np.arange(rows_dev)[None, :]
    phase = ((f * n) % (2 * rows_dev)) * (np.pi / rows_dev)
    fwd = np.zeros((2 * fp, rows_dev))
    fwd[:freqs] = np.cos(phase)
    fwd[fp : fp + freqs] = -np.sin(phase)
    t = np.arange(rows_dev)[:, None] + rows_dev
    f2 = np.arange(freqs)[None, :]
    phase2 = ((f2 * t) % (2 * rows_dev)) * (np.pi / rows_dev)
    weight = np.where((f2 == 0) | (f2 == rows_dev), 1.0, 2.0) / (2 * rows_dev)
    inv = np.zeros((rows_dev, 2 * fp))
    inv[:, :freqs] = weight * np.cos(phase2)
    inv[:, fp : fp + freqs] = -weight * np.sin(phase2)
    return fp, fwd, inv


def outer_tables(blocks, fp):
    size = 2 * blocks
    j = np.arange(blocks)[:, None]
    m = np.arange(size)[None, :]
    phase = 2 * np.pi * ((j * m) % size) / size
    fwd = np.concatenate([np.cos(phase), np.sin(phase)], axis=1)
    mi = np.arange(size)[:, None]
    i = np.arange(blocks)[None, :]
    phase_i = 2 * np.pi * ((mi * i) % size) / size
    cos_i = np.cos(phase_i) / size
    sin_i = np.sin(phase_i) / size
    inv_re = np.concatenate([cos_i, -sin_i], axis=0)
    inv_im = np.concatenate([sin_i, cos_i], axis=0)
    sign = np.where(np.arange(fp) % 2 == 0, 1.0, -1.0)[:, None]
    step = 2 * np.pi * np.arange(size)[None, :] / size
    return fwd, inv_re, inv_im, sign, np.cos(step), -np.sin(step)


def on_device(inputs, gate_values, causal_filter, anti_filter, skip_gain, norm_gain):
    rows_dev, chan_dev = inputs.shape
    blocks = lax.axis_size("seq")
    per = chan_dev // blocks
    size = 2 * blocks
    f32 = jnp.float32
    own_index = lax.axis_index("seq")

    fp, fwd_np, inv_np = inner_tables(rows_dev)
    ofwd_np, oinv_re_np, oinv_im_np, sign_np, cos_np, msin_np = outer_tables(blocks, fp)
    fwd = jnp.asarray(fwd_np, jnp.bfloat16)
    inv = jnp.asarray(inv_np, f32)
    ofwd = jnp.asarray(ofwd_np, f32)
    oinv = jnp.asarray(np.concatenate([oinv_re_np, oinv_im_np], axis=1), f32)
    sh_re = jnp.asarray(sign_np, f32) + jnp.asarray(cos_np, f32)
    sh_im = jnp.asarray(msin_np, f32)

    row_ids = lax.broadcasted_iota(jnp.int32, (rows_dev, 1), 0) + own_index * rows_dev
    anti_masked = jnp.where(row_ids > 0, anti_filter, jnp.zeros_like(anti_filter))
    stacked = jnp.stack([inputs, causal_filter, anti_masked, gate_values])
    lanes = 128
    eye_ch = jnp.eye(chan_dev, dtype=jnp.bfloat16)
    by_channel = jnp.einsum(
        "ck,atk->cat", eye_ch, stacked, preferred_element_type=f32
    ).astype(jnp.bfloat16)
    send = by_channel.reshape(blocks, per * 4 * rows_dev // lanes, lanes)
    recv = lax.all_to_all(send, "seq", 0, 0, tiled=True)
    series = recv.reshape(blocks, per, 4, rows_dev).transpose(0, 2, 1, 3)
    conv_in = series[:, :3].reshape(blocks, 3 * per, rows_dev).transpose(1, 0, 2)

    spec = jnp.einsum("fn,qbn->qfb", fwd, conv_in, preferred_element_type=f32)
    spec = spec.astype(jnp.bfloat16).astype(f32)
    z = jnp.einsum("qfb,bk->qfk", spec, ofwd, precision=HIGHEST, preferred_element_type=f32)
    z_re, z_im = z[:, :fp], z[:, fp:]
    x_re = (z_re[..., :size] + z_im[..., size:]).reshape(3, per, fp, size)
    x_im = (z_im[..., :size] - z_re[..., size:]).reshape(3, per, fp, size)

    c_re = sh_re * x_re[1] - sh_im * x_im[1]
    c_im = sh_re * x_im[1] + sh_im * x_re[1]
    a_re = sh_re * x_re[2] - sh_im * x_im[2]
    a_im = sh_re * x_im[2] + sh_im * x_re[2]
    k_re = c_re + a_re
    k_im = c_im - a_im
    y_re = k_re * x_re[0] - k_im * x_im[0]
    y_im = k_re * x_im[0] + k_im * x_re[0]
    y_cat = jnp.concatenate([y_re, y_im], axis=-1)

    t_both = jnp.einsum("cfk,ki->cfi", y_cat, oinv, precision=HIGHEST, preferred_element_type=f32)
    total = jnp.concatenate([t_both[..., :blocks], t_both[..., blocks:]], axis=1)
    conv_t = jnp.einsum("cfi,tf->ict", total, inv, precision=HIGH, preferred_element_type=f32)

    skip_here = lax.dynamic_slice_in_dim(skip_gain, own_index * per, per)
    mixed_local = series[:, 3].astype(f32) * (
        conv_t + skip_here[None, :, None] * series[:, 0].astype(f32)
    )
    back = mixed_local.reshape(blocks, per * rows_dev // lanes, lanes)
    got = lax.all_to_all(back, "seq", 0, 0, tiled=True)
    mix_t = got.reshape(blocks * per, rows_dev)

    partial = jnp.sum(mix_t * mix_t, axis=0)
    squares = jnp.sum(lax.all_gather(partial, "ch", axis=0, tiled=False), axis=0)
    inv_norm = lax.rsqrt(squares / D + 1e-06)
    out_t = (norm_gain[:, None] * mix_t * inv_norm[None, :]).astype(jnp.bfloat16)
    eye_tok = jnp.eye(rows_dev, dtype=jnp.bfloat16)
    return jnp.einsum("tk,ck->tc", eye_tok, out_t, preferred_element_type=f32).astype(
        jnp.bfloat16
    )


def solution(mesh):
    placed = (P("seq", "ch"), P("seq", "ch"), P("seq", "ch"), P("seq", "ch"), P("ch"), P("ch"))
    return jax.shard_map(
        on_device, mesh=mesh, in_specs=placed, out_specs=P("seq", "ch"), check_vma=False
    )
```

```python
import numpy as np

import jax
import jax.numpy as jnp
from jax import lax
from jax.sharding import PartitionSpec as P

D = 1024
HIGHEST = lax.Precision.HIGHEST
HIGH = lax.Precision.HIGH


def padded(count, unit=8):
    return -(-count // unit) * unit


def inner_tables(rows_dev):
    freqs = rows_dev + 1
    fp = padded(freqs)
    f = np.arange(freqs)[:, None]
    n = np.arange(rows_dev)[None, :]
    phase = ((f * n) % (2 * rows_dev)) * (np.pi / rows_dev)
    fwd = np.zeros((2 * fp, rows_dev))
    fwd[:freqs] = np.cos(phase)
    fwd[fp : fp + freqs] = -np.sin(phase)
    t = np.arange(rows_dev)[:, None] + rows_dev
    f2 = np.arange(freqs)[None, :]
    phase2 = ((f2 * t) % (2 * rows_dev)) * (np.pi / rows_dev)
    weight = np.where((f2 == 0) | (f2 == rows_dev), 1.0, 2.0) / (2 * rows_dev)
    inv = np.zeros((rows_dev, 2 * fp))
    inv[:, :freqs] = weight * np.cos(phase2)
    inv[:, fp : fp + freqs] = -weight * np.sin(phase2)
    return fp, fwd, inv


def outer_tables(blocks, fp):
    size = 2 * blocks
    j = np.arange(blocks)[:, None]
    m = np.arange(size)[None, :]
    phase = 2 * np.pi * ((j * m) % size) / size
    fwd = np.concatenate([np.cos(phase), np.sin(phase)], axis=1)
    mi = np.arange(size)[:, None]
    i = np.arange(blocks)[None, :]
    phase_i = 2 * np.pi * ((mi * i) % size) / size
    cos_i = np.cos(phase_i) / size
    sin_i = np.sin(phase_i) / size
    inv_re = np.concatenate([cos_i, -sin_i], axis=0)
    inv_im = np.concatenate([sin_i, cos_i], axis=0)
    sign = np.where(np.arange(fp) % 2 == 0, 1.0, -1.0)[:, None]
    step = 2 * np.pi * np.arange(size)[None, :] / size
    return fwd, inv_re, inv_im, sign, np.cos(step), -np.sin(step)


def on_device(inputs, gate_values, causal_filter, anti_filter, skip_gain, norm_gain):
    rows_dev, chan_dev = inputs.shape
    blocks = lax.axis_size("seq")
    per = chan_dev // blocks
    size = 2 * blocks
    f32 = jnp.float32
    own_index = lax.axis_index("seq")

    fp, fwd_np, inv_np = inner_tables(rows_dev)
    ofwd_np, oinv_re_np, oinv_im_np, sign_np, cos_np, msin_np = outer_tables(blocks, fp)
    fwd = jnp.asarray(fwd_np, jnp.bfloat16)
    inv = jnp.asarray(inv_np, f32)
    ofwd = jnp.asarray(ofwd_np, f32)
    oinv = jnp.asarray(np.concatenate([oinv_re_np, oinv_im_np], axis=1), f32)
    sh_re = jnp.asarray(sign_np, f32) + jnp.asarray(cos_np, f32)
    sh_im = jnp.asarray(msin_np, f32)

    stacked = jnp.stack([inputs, causal_filter, anti_filter, gate_values])
    lanes = 128
    eye_ch = jnp.eye(chan_dev, dtype=jnp.bfloat16)
    by_channel = jnp.einsum(
        "ck,atk->cat", eye_ch, stacked, preferred_element_type=f32
    ).astype(jnp.bfloat16)
    send = by_channel.reshape(blocks, per * 4 * rows_dev // lanes, lanes)
    recv = lax.all_to_all(send, "seq", 0, 0, tiled=True)
    series = recv.reshape(blocks, per, 4, rows_dev).transpose(0, 2, 1, 3)
    conv_in = series[:, :3].reshape(blocks, 3 * per, rows_dev).transpose(1, 0, 2)

    spec = jnp.einsum("fn,qbn->qfb", fwd, conv_in, preferred_element_type=f32)
    first_anti = series[0, 2, :, 0].astype(f32)
    q_ids = lax.broadcasted_iota(jnp.int32, (3 * per, 1, 1), 0)
    row0 = jnp.where(q_ids >= 2 * per, jnp.tile(first_anti, 3)[:, None, None], f32(0.0))
    col0 = fwd[:, 0].astype(f32)[None, :, None]
    at_first = (lax.broadcasted_iota(jnp.int32, (1, 1, blocks), 2) == 0).astype(f32)
    spec = spec - row0 * col0 * at_first
    spec = spec.astype(jnp.bfloat16).astype(f32)
    z = jnp.einsum("qfb,bk->qfk", spec, ofwd, precision=HIGHEST, preferred_element_type=f32)
    z_re, z_im = z[:, :fp], z[:, fp:]
    x_re = (z_re[..., :size] + z_im[..., size:]).reshape(3, per, fp, size)
    x_im = (z_im[..., :size] - z_re[..., size:]).reshape(3, per, fp, size)

    c_re = sh_re * x_re[1] - sh_im * x_im[1]
    c_im = sh_re * x_im[1] + sh_im * x_re[1]
    a_re = sh_re * x_re[2] - sh_im * x_im[2]
    a_im = sh_re * x_im[2] + sh_im * x_re[2]
    k_re = c_re + a_re
    k_im = c_im - a_im
    y_re = k_re * x_re[0] - k_im * x_im[0]
    y_im = k_re * x_im[0] + k_im * x_re[0]
    y_cat = jnp.concatenate([y_re, y_im], axis=-1)

    t_both = jnp.einsum("cfk,ki->cfi", y_cat, oinv, precision=HIGHEST, preferred_element_type=f32)
    total = jnp.concatenate([t_both[..., :blocks], t_both[..., blocks:]], axis=1)
    conv_t = jnp.einsum("cfi,tf->ict", total, inv, precision=HIGH, preferred_element_type=f32)

    skip_here = lax.dynamic_slice_in_dim(skip_gain, own_index * per, per)
    mixed_local = series[:, 3].astype(f32) * (
        conv_t + skip_here[None, :, None] * series[:, 0].astype(f32)
    )
    back = mixed_local.reshape(blocks, per * rows_dev // lanes, lanes)
    got = lax.all_to_all(back, "seq", 0, 0, tiled=True)
    mix_t = got.reshape(blocks * per, rows_dev)

    partial = jnp.sum(mix_t * mix_t, axis=0)
    squares = jnp.sum(lax.all_gather(partial, "ch", axis=0, tiled=False), axis=0)
    inv_norm = lax.rsqrt(squares / D + 1e-06)
    out_t = (norm_gain[:, None] * mix_t * inv_norm[None, :]).astype(jnp.bfloat16)
    eye_tok = jnp.eye(rows_dev, dtype=jnp.bfloat16)
    return jnp.einsum("tk,ck->tc", eye_tok, out_t, preferred_element_type=f32).astype(
        jnp.bfloat16
    )


def solution(mesh):
    placed = (P("seq", "ch"), P("seq", "ch"), P("seq", "ch"), P("seq", "ch"), P("ch"), P("ch"))
    return jax.shard_map(
        on_device, mesh=mesh, in_specs=placed, out_specs=P("seq", "ch"), check_vma=False
    )
```

```python
import numpy as np

import jax
import jax.numpy as jnp
from jax import lax
from jax.sharding import PartitionSpec as P

D = 1024
HIGHEST = lax.Precision.HIGHEST
HIGH = lax.Precision.HIGH


def padded(count, unit=8):
    return -(-count // unit) * unit


def inner_tables(rows_dev):
    freqs = rows_dev + 1
    fp = padded(freqs)
    f = np.arange(freqs)[:, None]
    n = np.arange(rows_dev)[None, :]
    phase = ((f * n) % (2 * rows_dev)) * (np.pi / rows_dev)
    fwd = np.zeros((2 * fp, rows_dev))
    fwd[:freqs] = np.cos(phase)
    fwd[fp : fp + freqs] = -np.sin(phase)
    t = np.arange(rows_dev)[:, None] + rows_dev
    f2 = np.arange(freqs)[None, :]
    phase2 = ((f2 * t) % (2 * rows_dev)) * (np.pi / rows_dev)
    weight = np.where((f2 == 0) | (f2 == rows_dev), 1.0, 2.0) / (2 * rows_dev)
    inv = np.zeros((rows_dev, 2 * fp))
    inv[:, :freqs] = weight * np.cos(phase2)
    inv[:, fp : fp + freqs] = -weight * np.sin(phase2)
    return fp, fwd, inv


def outer_tables(blocks, fp):
    size = 2 * blocks
    j = np.arange(blocks)[:, None]
    m = np.arange(size)[None, :]
    phase = 2 * np.pi * ((j * m) % size) / size
    fwd = np.concatenate([np.cos(phase), np.sin(phase)], axis=1)
    mi = np.arange(size)[:, None]
    i = np.arange(blocks)[None, :]
    phase_i = 2 * np.pi * ((mi * i) % size) / size
    cos_i = np.cos(phase_i) / size
    sin_i = np.sin(phase_i) / size
    inv_re = np.concatenate([cos_i, -sin_i], axis=0)
    inv_im = np.concatenate([sin_i, cos_i], axis=0)
    sign = np.where(np.arange(fp) % 2 == 0, 1.0, -1.0)[:, None]
    step = 2 * np.pi * np.arange(size)[None, :] / size
    return fwd, inv_re, inv_im, sign, np.cos(step), -np.sin(step)


def on_device(inputs, gate_values, causal_filter, anti_filter, skip_gain, norm_gain):
    rows_dev, chan_dev = inputs.shape
    blocks = lax.axis_size("seq")
    per = chan_dev // blocks
    size = 2 * blocks
    f32 = jnp.float32
    own_index = lax.axis_index("seq")

    fp, fwd_np, inv_np = inner_tables(rows_dev)
    ofwd_np, oinv_re_np, oinv_im_np, sign_np, cos_np, msin_np = outer_tables(blocks, fp)
    fwd = jnp.asarray(fwd_np, jnp.bfloat16)
    inv = jnp.asarray(inv_np, f32)
    ofwd = jnp.asarray(ofwd_np, f32)
    oinv = jnp.asarray(np.concatenate([oinv_re_np, oinv_im_np], axis=1), f32)
    parity = lax.broadcasted_iota(jnp.int32, (fp, 1), 0) % 2
    sh_re = (1 - 2 * parity).astype(f32) + ofwd[1:2, :size]
    sh_im = -ofwd[1:2, size:]

    stacked = jnp.stack([inputs, causal_filter, anti_filter, gate_values])
    lanes = 128
    eye_ch = jnp.eye(chan_dev, dtype=jnp.bfloat16)
    by_channel = jnp.einsum(
        "ck,atk->cat", eye_ch, stacked, preferred_element_type=f32
    ).astype(jnp.bfloat16)
    send = by_channel.reshape(blocks, per * 4 * rows_dev // lanes, lanes)
    recv = lax.all_to_all(send, "seq", 0, 0, tiled=True)
    series = recv.reshape(blocks, per, 4, rows_dev).transpose(0, 2, 1, 3)
    block_ids = lax.broadcasted_iota(jnp.int32, (blocks, 1, rows_dev), 0)
    tok_ids = lax.broadcasted_iota(jnp.int32, (blocks, 1, rows_dev), 2)
    first_row = jnp.logical_and(block_ids == 0, tok_ids == 0)
    anti_rows = jnp.where(first_row, jnp.zeros_like(series[:, 2]), series[:, 2])
    conv_in = jnp.stack([series[:, 0], series[:, 1], anti_rows], axis=1)
    conv_in = conv_in.reshape(blocks, 3 * per, rows_dev).transpose(1, 0, 2)

    spec = jnp.einsum("fn,qbn->qfb", fwd, conv_in, preferred_element_type=f32)
    spec = spec.astype(jnp.bfloat16).astype(f32)
    z = jnp.einsum("qfb,bk->qfk", spec, ofwd, precision=HIGHEST, preferred_element_type=f32)
    z_re, z_im = z[:, :fp], z[:, fp:]
    x_re = (z_re[..., :size] + z_im[..., size:]).reshape(3, per, fp, size)
    x_im = (z_im[..., :size] - z_re[..., size:]).reshape(3, per, fp, size)

    c_re = sh_re * x_re[1] - sh_im * x_im[1]
    c_im = sh_re * x_im[1] + sh_im * x_re[1]
    a_re = sh_re * x_re[2] - sh_im * x_im[2]
    a_im = sh_re * x_im[2] + sh_im * x_re[2]
    k_re = c_re + a_re
    k_im = c_im - a_im
    y_re = k_re * x_re[0] - k_im * x_im[0]
    y_im = k_re * x_im[0] + k_im * x_re[0]
    y_cat = jnp.concatenate([y_re, y_im], axis=-1)

    t_both = jnp.einsum("cfk,ki->cfi", y_cat, oinv, precision=HIGHEST, preferred_element_type=f32)
    total = jnp.concatenate([t_both[..., :blocks], t_both[..., blocks:]], axis=1)
    conv_t = jnp.einsum("cfi,tf->ict", total, inv, precision=HIGH, preferred_element_type=f32)

    skip_here = lax.dynamic_slice_in_dim(skip_gain, own_index * per, per)
    mixed_local = series[:, 3].astype(f32) * (
        conv_t + skip_here[None, :, None] * series[:, 0].astype(f32)
    )
    back = mixed_local.reshape(blocks, per * rows_dev // lanes, lanes)
    got = lax.all_to_all(back, "seq", 0, 0, tiled=True)
    mix_t = got.reshape(blocks * per, rows_dev)

    partial = jnp.sum(mix_t * mix_t, axis=0)
    squares = jnp.sum(lax.all_gather(partial, "ch", axis=0, tiled=False), axis=0)
    inv_norm = lax.rsqrt(squares / D + 1e-06)
    out_t = (norm_gain[:, None] * mix_t * inv_norm[None, :]).astype(jnp.bfloat16)
    eye_tok = jnp.eye(rows_dev, dtype=jnp.bfloat16)
    return jnp.einsum("tk,ck->tc", eye_tok, out_t, preferred_element_type=f32).astype(
        jnp.bfloat16
    )


def solution(mesh):
    placed = (P("seq", "ch"), P("seq", "ch"), P("seq", "ch"), P("seq", "ch"), P("ch"), P("ch"))
    return jax.shard_map(
        on_device, mesh=mesh, in_specs=placed, out_specs=P("seq", "ch"), check_vma=False
    )
```

```python
import numpy as np

import jax
import jax.numpy as jnp
from jax import lax
from jax.sharding import PartitionSpec as P

D = 1024
HIGHEST = lax.Precision.HIGHEST
HIGH = lax.Precision.HIGH


def padded(count, unit=8):
    return -(-count // unit) * unit


def inner_tables(rows_dev):
    freqs = rows_dev + 1
    fp = padded(freqs)
    f = np.arange(freqs)[:, None]
    n = np.arange(rows_dev)[None, :]
    phase = ((f * n) % (2 * rows_dev)) * (np.pi / rows_dev)
    fwd = np.zeros((2 * fp, rows_dev))
    fwd[:freqs] = np.cos(phase)
    fwd[fp : fp + freqs] = -np.sin(phase)
    t = np.arange(rows_dev)[:, None] + rows_dev
    f2 = np.arange(freqs)[None, :]
    phase2 = ((f2 * t) % (2 * rows_dev)) * (np.pi / rows_dev)
    weight = np.where((f2 == 0) | (f2 == rows_dev), 1.0, 2.0) / (2 * rows_dev)
    inv = np.zeros((rows_dev, 2 * fp))
    inv[:, :freqs] = weight * np.cos(phase2)
    inv[:, fp : fp + freqs] = -weight * np.sin(phase2)
    return fp, fwd, inv


def outer_tables(blocks, fp):
    size = 2 * blocks
    j = np.arange(blocks)[:, None]
    m = np.arange(size)[None, :]
    phase = 2 * np.pi * ((j * m) % size) / size
    fwd = np.concatenate([np.cos(phase), np.sin(phase)], axis=1)
    mi = np.arange(size)[:, None]
    i = np.arange(blocks)[None, :]
    phase_i = 2 * np.pi * ((mi * i) % size) / size
    cos_i = np.cos(phase_i) / size
    sin_i = np.sin(phase_i) / size
    inv_re = np.concatenate([cos_i, -sin_i], axis=0)
    inv_im = np.concatenate([sin_i, cos_i], axis=0)
    sign = np.where(np.arange(fp) % 2 == 0, 1.0, -1.0)[:, None]
    step = 2 * np.pi * np.arange(size)[None, :] / size
    return fwd, inv_re, inv_im, sign, np.cos(step), -np.sin(step)


def on_device(inputs, gate_values, causal_filter, anti_filter, skip_gain, norm_gain):
    rows_dev, chan_dev = inputs.shape
    blocks = lax.axis_size("seq")
    per = chan_dev // blocks
    size = 2 * blocks
    f32 = jnp.float32
    own_index = lax.axis_index("seq")

    fp, fwd_np, inv_np = inner_tables(rows_dev)
    ofwd_np, oinv_re_np, oinv_im_np, sign_np, cos_np, msin_np = outer_tables(blocks, fp)
    fwd = jnp.asarray(fwd_np, jnp.bfloat16)
    inv = jnp.asarray(inv_np, f32)
    ofwd = jnp.asarray(ofwd_np, f32)
    oinv = jnp.asarray(np.concatenate([oinv_re_np, oinv_im_np], axis=1), f32)
    parity = lax.broadcasted_iota(jnp.int32, (fp, 1), 0) % 2
    zero = f32(0.0) * own_index.astype(f32)
    sh_re = (1 - 2 * parity).astype(f32) + (ofwd[1:2, :size] + zero)
    sh_im = -(ofwd[1:2, size:] + zero)

    stacked = jnp.stack([inputs, causal_filter, anti_filter, gate_values])
    lanes = 128
    eye_ch = jnp.eye(chan_dev, dtype=jnp.bfloat16)
    by_channel = jnp.einsum(
        "ck,atk->cat", eye_ch, stacked, preferred_element_type=f32
    ).astype(jnp.bfloat16)
    send = by_channel.reshape(blocks, per * 4 * rows_dev // lanes, lanes)
    recv = lax.all_to_all(send, "seq", 0, 0, tiled=True)
    series = recv.reshape(blocks, per, 4, rows_dev).transpose(0, 2, 1, 3)
    block_ids = lax.broadcasted_iota(jnp.int32, (blocks, 1, rows_dev), 0)
    tok_ids = lax.broadcasted_iota(jnp.int32, (blocks, 1, rows_dev), 2)
    first_row = jnp.logical_and(block_ids == 0, tok_ids == 0)
    anti_rows = jnp.where(first_row, jnp.zeros_like(series[:, 2]), series[:, 2])
    conv_in = jnp.stack([series[:, 0], series[:, 1], anti_rows], axis=1)
    conv_in = conv_in.reshape(blocks, 3 * per, rows_dev).transpose(1, 0, 2)

    spec = jnp.einsum("fn,qbn->qfb", fwd, conv_in, preferred_element_type=f32)
    spec = spec.astype(jnp.bfloat16).astype(f32)
    z = jnp.einsum("qfb,bk->qfk", spec, ofwd, precision=HIGHEST, preferred_element_type=f32)
    z_re, z_im = z[:, :fp], z[:, fp:]
    x_re = (z_re[..., :size] + z_im[..., size:]).reshape(3, per, fp, size)
    x_im = (z_im[..., :size] - z_re[..., size:]).reshape(3, per, fp, size)

    c_re = sh_re * x_re[1] - sh_im * x_im[1]
    c_im = sh_re * x_im[1] + sh_im * x_re[1]
    a_re = sh_re * x_re[2] - sh_im * x_im[2]
    a_im = sh_re * x_im[2] + sh_im * x_re[2]
    k_re = c_re + a_re
    k_im = c_im - a_im
    y_re = k_re * x_re[0] - k_im * x_im[0]
    y_im = k_re * x_im[0] + k_im * x_re[0]
    y_cat = jnp.concatenate([y_re, y_im], axis=-1)

    t_both = jnp.einsum("cfk,ki->cfi", y_cat, oinv, precision=HIGHEST, preferred_element_type=f32)
    total = jnp.concatenate([t_both[..., :blocks], t_both[..., blocks:]], axis=1)
    conv_t = jnp.einsum("cfi,tf->ict", total, inv, precision=HIGH, preferred_element_type=f32)

    skip_here = lax.dynamic_slice_in_dim(skip_gain, own_index * per, per)
    mixed_local = series[:, 3].astype(f32) * (
        conv_t + skip_here[None, :, None] * series[:, 0].astype(f32)
    )
    back = mixed_local.reshape(blocks, per * rows_dev // lanes, lanes)
    got = lax.all_to_all(back, "seq", 0, 0, tiled=True)
    mix_t = got.reshape(blocks * per, rows_dev)

    partial = jnp.sum(mix_t * mix_t, axis=0)
    squares = jnp.sum(lax.all_gather(partial, "ch", axis=0, tiled=False), axis=0)
    inv_norm = lax.rsqrt(squares / D + 1e-06)
    out_t = (norm_gain[:, None] * mix_t * inv_norm[None, :]).astype(jnp.bfloat16)
    eye_tok = jnp.eye(rows_dev, dtype=jnp.bfloat16)
    return jnp.einsum("tk,ck->tc", eye_tok, out_t, preferred_element_type=f32).astype(
        jnp.bfloat16
    )


def solution(mesh):
    placed = (P("seq", "ch"), P("seq", "ch"), P("seq", "ch"), P("seq", "ch"), P("ch"), P("ch"))
    return jax.shard_map(
        on_device, mesh=mesh, in_specs=placed, out_specs=P("seq", "ch"), check_vma=False
    )
```

```python
import numpy as np

import jax
import jax.numpy as jnp
from jax import lax
from jax.sharding import PartitionSpec as P

D = 1024
HIGHEST = lax.Precision.HIGHEST
HIGH = lax.Precision.HIGH


def padded(count, unit=8):
    return -(-count // unit) * unit


def inner_tables(rows_dev):
    freqs = rows_dev + 1
    fp = padded(freqs)
    f = np.arange(freqs)[:, None]
    n = np.arange(rows_dev)[None, :]
    phase = ((f * n) % (2 * rows_dev)) * (np.pi / rows_dev)
    fwd = np.zeros((2 * fp, rows_dev))
    fwd[:freqs] = np.cos(phase)
    fwd[fp : fp + freqs] = -np.sin(phase)
    t = np.arange(rows_dev)[:, None] + rows_dev
    f2 = np.arange(freqs)[None, :]
    phase2 = ((f2 * t) % (2 * rows_dev)) * (np.pi / rows_dev)
    weight = np.where((f2 == 0) | (f2 == rows_dev), 1.0, 2.0) / (2 * rows_dev)
    inv = np.zeros((rows_dev, 2 * fp))
    inv[:, :freqs] = weight * np.cos(phase2)
    inv[:, fp : fp + freqs] = -weight * np.sin(phase2)
    return fp, fwd, inv


def outer_tables(blocks, fp):
    size = 2 * blocks
    j = np.arange(blocks)[:, None]
    m = np.arange(size)[None, :]
    phase = 2 * np.pi * ((j * m) % size) / size
    fwd = np.concatenate([np.cos(phase), np.sin(phase)], axis=1)
    mi = np.arange(size)[:, None]
    i = np.arange(blocks)[None, :]
    phase_i = 2 * np.pi * ((mi * i) % size) / size
    cos_i = np.cos(phase_i) / size
    sin_i = np.sin(phase_i) / size
    inv_re = np.concatenate([cos_i, -sin_i], axis=0)
    inv_im = np.concatenate([sin_i, cos_i], axis=0)
    sign = np.where(np.arange(fp) % 2 == 0, 1.0, -1.0)[:, None]
    step = 2 * np.pi * np.arange(size)[None, :] / size
    return fwd, inv_re, inv_im, sign, np.cos(step), -np.sin(step)


def on_device(inputs, gate_values, causal_filter, anti_filter, skip_gain, norm_gain):
    rows_dev, chan_dev = inputs.shape
    blocks = lax.axis_size("seq")
    per = chan_dev // blocks
    size = 2 * blocks
    f32 = jnp.float32
    own_index = lax.axis_index("seq")

    fp, fwd_np, inv_np = inner_tables(rows_dev)
    ofwd_np, oinv_re_np, oinv_im_np, sign_np, cos_np, msin_np = outer_tables(blocks, fp)
    fwd = jnp.asarray(fwd_np, jnp.bfloat16)
    inv = jnp.asarray(inv_np, f32)
    ofwd = jnp.asarray(ofwd_np, f32)
    zero_t = f32(0.0) * own_index.astype(f32)
    cos_t = (ofwd[:, :size] + zero_t).T / f32(size)
    sin_t = (ofwd[:, size:] + zero_t).T / f32(size)
    oinv = jnp.concatenate(
        [jnp.concatenate([cos_t, sin_t], axis=1), jnp.concatenate([-sin_t, cos_t], axis=1)], axis=0
    )
    parity = lax.broadcasted_iota(jnp.int32, (fp, 1), 0) % 2
    zero = f32(0.0) * own_index.astype(f32)
    sh_re = (1 - 2 * parity).astype(f32) + (ofwd[1:2, :size] + zero)
    sh_im = -(ofwd[1:2, size:] + zero)

    stacked = jnp.stack([inputs, causal_filter, anti_filter, gate_values])
    lanes = 128
    eye_ch = jnp.eye(chan_dev, dtype=jnp.bfloat16)
    by_channel = jnp.einsum(
        "ck,atk->cat", eye_ch, stacked, preferred_element_type=f32
    ).astype(jnp.bfloat16)
    send = by_channel.reshape(blocks, per * 4 * rows_dev // lanes, lanes)
    recv = lax.all_to_all(send, "seq", 0, 0, tiled=True)
    series = recv.reshape(blocks, per, 4, rows_dev).transpose(0, 2, 1, 3)
    block_ids = lax.broadcasted_iota(jnp.int32, (blocks, 1, rows_dev), 0)
    tok_ids = lax.broadcasted_iota(jnp.int32, (blocks, 1, rows_dev), 2)
    first_row = jnp.logical_and(block_ids == 0, tok_ids == 0)
    anti_rows = jnp.where(first_row, jnp.zeros_like(series[:, 2]), series[:, 2])
    conv_in = jnp.stack([series[:, 0], series[:, 1], anti_rows], axis=1)
    conv_in = conv_in.reshape(blocks, 3 * per, rows_dev).transpose(1, 0, 2)

    spec = jnp.einsum("fn,qbn->qfb", fwd, conv_in, preferred_element_type=f32)
    spec = spec.astype(jnp.bfloat16).astype(f32)
    z = jnp.einsum("qfb,bk->qfk", spec, ofwd, precision=HIGHEST, preferred_element_type=f32)
    z_re, z_im = z[:, :fp], z[:, fp:]
    x_re = (z_re[..., :size] + z_im[..., size:]).reshape(3, per, fp, size)
    x_im = (z_im[..., :size] - z_re[..., size:]).reshape(3, per, fp, size)

    c_re = sh_re * x_re[1] - sh_im * x_im[1]
    c_im = sh_re * x_im[1] + sh_im * x_re[1]
    a_re = sh_re * x_re[2] - sh_im * x_im[2]
    a_im = sh_re * x_im[2] + sh_im * x_re[2]
    k_re = c_re + a_re
    k_im = c_im - a_im
    y_re = k_re * x_re[0] - k_im * x_im[0]
    y_im = k_re * x_im[0] + k_im * x_re[0]
    y_cat = jnp.concatenate([y_re, y_im], axis=-1)

    t_both = jnp.einsum("cfk,ki->cfi", y_cat, oinv, precision=HIGHEST, preferred_element_type=f32)
    total = jnp.concatenate([t_both[..., :blocks], t_both[..., blocks:]], axis=1)
    conv_t = jnp.einsum("cfi,tf->ict", total, inv, precision=HIGH, preferred_element_type=f32)

    skip_here = lax.dynamic_slice_in_dim(skip_gain, own_index * per, per)
    mixed_local = series[:, 3].astype(f32) * (
        conv_t + skip_here[None, :, None] * series[:, 0].astype(f32)
    )
    back = mixed_local.reshape(blocks, per * rows_dev // lanes, lanes)
    got = lax.all_to_all(back, "seq", 0, 0, tiled=True)
    mix_t = got.reshape(blocks * per, rows_dev)

    partial = jnp.sum(mix_t * mix_t, axis=0)
    squares = jnp.sum(lax.all_gather(partial, "ch", axis=0, tiled=False), axis=0)
    inv_norm = lax.rsqrt(squares / D + 1e-06)
    out_t = (norm_gain[:, None] * mix_t * inv_norm[None, :]).astype(jnp.bfloat16)
    eye_tok = jnp.eye(rows_dev, dtype=jnp.bfloat16)
    return jnp.einsum("tk,ck->tc", eye_tok, out_t, preferred_element_type=f32).astype(
        jnp.bfloat16
    )


def solution(mesh):
    placed = (P("seq", "ch"), P("seq", "ch"), P("seq", "ch"), P("seq", "ch"), P("ch"), P("ch"))
    return jax.shard_map(
        on_device, mesh=mesh, in_specs=placed, out_specs=P("seq", "ch"), check_vma=False
    )
```

```python
import numpy as np

import jax
import jax.numpy as jnp
from jax import lax
from jax.sharding import PartitionSpec as P

D = 1024
HIGHEST = lax.Precision.HIGHEST
HIGH = lax.Precision.HIGH


def padded(count, unit=8):
    return -(-count // unit) * unit


def inner_tables(rows_dev):
    freqs = rows_dev + 1
    fp = padded(freqs)
    f = np.arange(freqs)[:, None]
    n = np.arange(rows_dev)[None, :]
    phase = ((f * n) % (2 * rows_dev)) * (np.pi / rows_dev)
    fwd = np.zeros((2 * fp, rows_dev))
    fwd[:freqs] = np.cos(phase)
    fwd[fp : fp + freqs] = -np.sin(phase)
    t = np.arange(rows_dev)[:, None] + rows_dev
    f2 = np.arange(freqs)[None, :]
    phase2 = ((f2 * t) % (2 * rows_dev)) * (np.pi / rows_dev)
    weight = np.where((f2 == 0) | (f2 == rows_dev), 1.0, 2.0) / (2 * rows_dev)
    inv = np.zeros((rows_dev, 2 * fp))
    inv[:, :freqs] = weight * np.cos(phase2)
    inv[:, fp : fp + freqs] = -weight * np.sin(phase2)
    return fp, fwd, inv


def outer_tables(blocks, fp):
    size = 2 * blocks
    j = np.arange(blocks)[:, None]
    m = np.arange(size)[None, :]
    phase = 2 * np.pi * ((j * m) % size) / size
    fwd = np.concatenate([np.cos(phase), np.sin(phase)], axis=1)
    mi = np.arange(size)[:, None]
    i = np.arange(blocks)[None, :]
    phase_i = 2 * np.pi * ((mi * i) % size) / size
    cos_i = np.cos(phase_i) / size
    sin_i = np.sin(phase_i) / size
    inv_re = np.concatenate([cos_i, -sin_i], axis=0)
    inv_im = np.concatenate([sin_i, cos_i], axis=0)
    sign = np.where(np.arange(fp) % 2 == 0, 1.0, -1.0)[:, None]
    step = 2 * np.pi * np.arange(size)[None, :] / size
    return fwd, inv_re, inv_im, sign, np.cos(step), -np.sin(step)


def on_device(inputs, gate_values, causal_filter, anti_filter, skip_gain, norm_gain):
    rows_dev, chan_dev = inputs.shape
    blocks = lax.axis_size("seq")
    per = chan_dev // blocks
    size = 2 * blocks
    f32 = jnp.float32
    own_index = lax.axis_index("seq")

    fp, fwd_np, inv_np = inner_tables(rows_dev)
    ofwd_np, oinv_re_np, oinv_im_np, sign_np, cos_np, msin_np = outer_tables(blocks, fp)
    fwd = jnp.asarray(fwd_np, jnp.bfloat16)
    inv = jnp.asarray(inv_np, f32)
    ofwd = jnp.asarray(ofwd_np, f32)
    zero_t = f32(0.0) * own_index.astype(f32)
    cos_t = (ofwd[:, :size] + zero_t).T / f32(size)
    sin_t = (ofwd[:, size:] + zero_t).T / f32(size)
    oinv = jnp.concatenate(
        [jnp.concatenate([cos_t, sin_t], axis=1), jnp.concatenate([-sin_t, cos_t], axis=1)], axis=0
    )
    parity = lax.broadcasted_iota(jnp.int32, (fp, 1), 0) % 2
    zero = f32(0.0) * own_index.astype(f32)
    sh_re = (1 - 2 * parity).astype(f32) + (ofwd[1:2, :size] + zero)
    sh_im = -(ofwd[1:2, size:] + zero)

    stacked = jnp.stack([inputs, causal_filter, anti_filter, gate_values])
    lanes = 128
    eye_ch = jnp.eye(chan_dev, dtype=jnp.bfloat16)
    by_channel = jnp.einsum(
        "ck,atk->cat", eye_ch, stacked, preferred_element_type=f32
    ).astype(jnp.bfloat16)
    send = by_channel.reshape(blocks, per * 4 * rows_dev // lanes, lanes)
    recv = lax.all_to_all(send, "seq", 0, 0, tiled=True)
    series = recv.reshape(blocks, per, 4, rows_dev).transpose(0, 2, 1, 3)
    block_ids = lax.broadcasted_iota(jnp.int32, (blocks, 1, rows_dev), 0)
    tok_ids = lax.broadcasted_iota(jnp.int32, (blocks, 1, rows_dev), 2)
    first_row = jnp.logical_and(block_ids == 0, tok_ids == 0)
    anti_rows = jnp.where(first_row, jnp.zeros_like(series[:, 2]), series[:, 2])
    conv_in = jnp.stack([series[:, 0], series[:, 1], anti_rows], axis=1)
    conv_in = conv_in.reshape(blocks, 3 * per, rows_dev).transpose(1, 0, 2)

    spec = jnp.einsum("fn,qbn->qfb", fwd, conv_in, preferred_element_type=f32)
    spec = spec.astype(jnp.bfloat16).astype(f32)
    z = jnp.einsum("qfb,bk->qfk", spec, ofwd, precision=HIGHEST, preferred_element_type=f32)
    z_re, z_im = z[:, :fp], z[:, fp:]
    x_re = (z_re[..., :size] + z_im[..., size:]).reshape(3, per, fp, size)
    x_im = (z_im[..., :size] - z_re[..., size:]).reshape(3, per, fp, size)

    c_re = sh_re * x_re[1] - sh_im * x_im[1]
    c_im = sh_re * x_im[1] + sh_im * x_re[1]
    a_re = sh_re * x_re[2] - sh_im * x_im[2]
    a_im = sh_re * x_im[2] + sh_im * x_re[2]
    k_re = c_re + a_re
    k_im = c_im - a_im
    y_re = k_re * x_re[0] - k_im * x_im[0]
    y_im = k_re * x_im[0] + k_im * x_re[0]
    y_cat = jnp.concatenate([y_re, y_im], axis=-1)

    t_both = jnp.einsum("cfk,ki->cfi", y_cat, oinv, precision=HIGHEST, preferred_element_type=f32)
    total = jnp.concatenate([t_both[..., :blocks], t_both[..., blocks:]], axis=1)
    conv_t = jnp.einsum("cfi,tf->ict", total, inv, precision=HIGH, preferred_element_type=f32)

    skip_here = lax.dynamic_slice_in_dim(skip_gain, own_index * per, per)
    mixed_local = series[:, 3].astype(f32) * (
        conv_t + skip_here[None, :, None] * series[:, 0].astype(f32)
    )
    got = lax.all_to_all(mixed_local, "seq", 0, 0, tiled=True)
    mix_t = got.reshape(blocks * per, rows_dev)

    partial = jnp.sum(mix_t * mix_t, axis=0)
    squares = jnp.sum(lax.all_gather(partial, "ch", axis=0, tiled=False), axis=0)
    inv_norm = lax.rsqrt(squares / D + 1e-06)
    out_t = (norm_gain[:, None] * mix_t * inv_norm[None, :]).astype(jnp.bfloat16)
    eye_tok = jnp.eye(rows_dev, dtype=jnp.bfloat16)
    return jnp.einsum("tk,ck->tc", eye_tok, out_t, preferred_element_type=f32).astype(
        jnp.bfloat16
    )


def solution(mesh):
    placed = (P("seq", "ch"), P("seq", "ch"), P("seq", "ch"), P("seq", "ch"), P("ch"), P("ch"))
    return jax.shard_map(
        on_device, mesh=mesh, in_specs=placed, out_specs=P("seq", "ch"), check_vma=False
    )
```

```python
import numpy as np

import jax
import jax.numpy as jnp
from jax import lax
from jax.sharding import PartitionSpec as P

D = 1024
HIGHEST = lax.Precision.HIGHEST
HIGH = lax.Precision.HIGH


def padded(count, unit=8):
    return -(-count // unit) * unit


def inner_tables(rows_dev):
    freqs = rows_dev + 1
    fp = padded(freqs)
    f = np.arange(freqs)[:, None]
    n = np.arange(rows_dev)[None, :]
    phase = ((f * n) % (2 * rows_dev)) * (np.pi / rows_dev)
    fwd = np.zeros((2 * fp, rows_dev))
    fwd[:freqs] = np.cos(phase)
    fwd[fp : fp + freqs] = -np.sin(phase)
    t = np.arange(rows_dev)[:, None] + rows_dev
    f2 = np.arange(freqs)[None, :]
    phase2 = ((f2 * t) % (2 * rows_dev)) * (np.pi / rows_dev)
    weight = np.where((f2 == 0) | (f2 == rows_dev), 1.0, 2.0) / (2 * rows_dev)
    inv = np.zeros((rows_dev, 2 * fp))
    inv[:, :freqs] = weight * np.cos(phase2)
    inv[:, fp : fp + freqs] = -weight * np.sin(phase2)
    return fp, fwd, inv


def outer_tables(blocks, fp):
    size = 2 * blocks
    j = np.arange(blocks)[:, None]
    m = np.arange(size)[None, :]
    phase = 2 * np.pi * ((j * m) % size) / size
    fwd = np.concatenate([np.cos(phase), np.sin(phase)], axis=1)
    mi = np.arange(size)[:, None]
    i = np.arange(blocks)[None, :]
    phase_i = 2 * np.pi * ((mi * i) % size) / size
    cos_i = np.cos(phase_i) / size
    sin_i = np.sin(phase_i) / size
    inv_re = np.concatenate([cos_i, -sin_i], axis=0)
    inv_im = np.concatenate([sin_i, cos_i], axis=0)
    sign = np.where(np.arange(fp) % 2 == 0, 1.0, -1.0)[:, None]
    step = 2 * np.pi * np.arange(size)[None, :] / size
    return fwd, inv_re, inv_im, sign, np.cos(step), -np.sin(step)


def on_device(inputs, gate_values, causal_filter, anti_filter, skip_gain, norm_gain):
    rows_dev, chan_dev = inputs.shape
    blocks = lax.axis_size("seq")
    per = chan_dev // blocks
    size = 2 * blocks
    f32 = jnp.float32
    own_index = lax.axis_index("seq")

    fp, fwd_np, inv_np = inner_tables(rows_dev)
    ofwd_np, oinv_re_np, oinv_im_np, sign_np, cos_np, msin_np = outer_tables(blocks, fp)
    fwd = jnp.asarray(fwd_np, jnp.bfloat16)
    inv = jnp.asarray(inv_np, f32)
    ofwd = jnp.asarray(ofwd_np, f32)
    zero_t = f32(0.0) * own_index.astype(f32)
    cos_t = (ofwd[:, :size] + zero_t).T / f32(size)
    sin_t = (ofwd[:, size:] + zero_t).T / f32(size)
    oinv = jnp.concatenate(
        [jnp.concatenate([cos_t, sin_t], axis=1), jnp.concatenate([-sin_t, cos_t], axis=1)], axis=0
    )
    parity = lax.broadcasted_iota(jnp.int32, (fp, 1), 0) % 2
    zero = f32(0.0) * own_index.astype(f32)
    sh_re = (1 - 2 * parity).astype(f32) + (ofwd[1:2, :size] + zero)
    sh_im = -(ofwd[1:2, size:] + zero)

    stacked = jnp.stack([inputs, causal_filter, anti_filter, gate_values])
    lanes = 128
    eye_ch = jnp.eye(chan_dev, dtype=jnp.bfloat16)
    by_channel = jnp.einsum(
        "ck,atk->cat", eye_ch, stacked, preferred_element_type=f32
    ).astype(jnp.bfloat16)
    send = by_channel.reshape(blocks, per * 4 * rows_dev // lanes, lanes)
    recv = lax.all_to_all(send, "seq", 0, 0, tiled=True)
    series = recv.reshape(blocks, per, 4, rows_dev).transpose(0, 2, 1, 3)
    block_ids = lax.broadcasted_iota(jnp.int32, (blocks, 1, rows_dev), 0)
    tok_ids = lax.broadcasted_iota(jnp.int32, (blocks, 1, rows_dev), 2)
    first_row = jnp.logical_and(block_ids == 0, tok_ids == 0)
    anti_rows = jnp.where(first_row, jnp.zeros_like(series[:, 2]), series[:, 2])
    conv_in = jnp.stack([series[:, 0], series[:, 1], anti_rows], axis=1)
    conv_in = conv_in.reshape(blocks, 3 * per, rows_dev).transpose(1, 0, 2)

    spec = jnp.einsum("fn,qbn->qfb", fwd, conv_in, preferred_element_type=f32)
    spec = spec.astype(jnp.bfloat16).astype(f32)
    z = jnp.einsum("qfb,bk->qfk", spec, ofwd, precision=HIGHEST, preferred_element_type=f32)
    z_re, z_im = z[:, :fp], z[:, fp:]
    x_re = (z_re[..., :size] + z_im[..., size:]).reshape(3, per, fp, size)
    x_im = (z_im[..., :size] - z_re[..., size:]).reshape(3, per, fp, size)

    c_re = sh_re * x_re[1] - sh_im * x_im[1]
    c_im = sh_re * x_im[1] + sh_im * x_re[1]
    a_re = sh_re * x_re[2] - sh_im * x_im[2]
    a_im = sh_re * x_im[2] + sh_im * x_re[2]
    k_re = c_re + a_re
    k_im = c_im - a_im
    y_re = k_re * x_re[0] - k_im * x_im[0]
    y_im = k_re * x_im[0] + k_im * x_re[0]
    y_cat = jnp.concatenate([y_re, y_im], axis=-1)

    t_both = jnp.einsum("cfk,ki->cfi", y_cat, oinv, precision=HIGHEST, preferred_element_type=f32)
    total = jnp.concatenate([t_both[..., :blocks], t_both[..., blocks:]], axis=1)
    conv_t = jnp.einsum("cfi,tf->ict", total, inv, precision=HIGH, preferred_element_type=f32)

    skip_here = lax.dynamic_slice_in_dim(skip_gain, own_index * per, per)
    mixed_local = series[:, 3].astype(f32) * (
        conv_t + skip_here[None, :, None] * series[:, 0].astype(f32)
    )
    got = lax.all_to_all(mixed_local, "seq", 0, 0, tiled=True)
    mix_t = got.reshape(blocks * per, rows_dev)

    partial = jnp.sum(mix_t * mix_t, axis=0)
    squares = jnp.sum(lax.all_gather(partial, "ch", axis=0, tiled=False), axis=0)
    inv_norm = lax.rsqrt(squares / D + 1e-06)
    out_t = (norm_gain[:, None] * mix_t * inv_norm[None, :]).astype(jnp.bfloat16)
    return out_t.T


def solution(mesh):
    placed = (P("seq", "ch"), P("seq", "ch"), P("seq", "ch"), P("seq", "ch"), P("ch"), P("ch"))
    return jax.shard_map(
        on_device, mesh=mesh, in_specs=placed, out_specs=P("seq", "ch"), check_vma=False
    )
```
